32 devices in a mesh: ctx: 16 (over z, y, core), head: 2 (over x).
Axes of the slice: x: 2, y: 2, z: 4, core: 2. Of those that a mesh axis runs over, the one named last changes fastest.
Arguments:
- queries: bfloat16 [2048, 1536], P('ctx', 'head'), may hold values from -45 to 45
- key_rows: bfloat16 [2048, 256], P('ctx', 'head'), may hold values from -5 to 5
- value_rows: bfloat16 [2048, 256], P('ctx', 'head'), may hold values from -18 to 18
- cotangent: bfloat16 [2048, 1536], P('ctx', 'head'), may hold values from -6 to 6
- trace_ids: int32 [2048], P('ctx'), may hold values from 0 to 15, never falling along the last dimension, each value on 1 to 512 neighbouring positions
- correct: int32 [16], replicated, may hold values from 0 to 16, as said below
- group_size: int32 [16], replicated, may hold values from 4 to 16
Outputs:
- log_totals: float32 [2048, 12], P('ctx', 'head')
- grad_queries: float32 [2048, 1536], P('ctx', 'head')
- grad_keys: bfloat16 [2048, 256], P('ctx', 'head')
- grad_values: bfloat16 [2048, 256], P('ctx', 'head')
The draws below stay inside these ranges and needn't reach their ends.
Inputs may be any that keep to these rules, and one draw needn't show every extreme that they name: correct[g] is at most group_size[g].
All inputs are finite; a program needn't handle non-finite values.
Results may differ from the reference program's by a relative error of at most 0.0054.
Values may be sent and summed in bfloat16 or wider, within the bound.
No kernel may reach another device: no remote copies, remote signals or barrier semaphores. Data moves between devices by JAX's collectives and lax.ppermute only.
A program may use at most 64 MiB of HBM per device.

```python
import math
import jax
import jax.numpy as jnp
import numpy as np
from jax import lax

HD = 128
QH = 6
KV_HEADS = 2
TOKENS = 2048
TRACES = 16
PASSK = 4
NMAX = 16


def key_field(key):
    base_key = jax.random.fold_in(key, 11)
    field = jax.random.truncated_normal(base_key, -4.5, 4.5, (TOKENS, KV_HEADS * HD), jnp.float32)
    return field


def draw_key_rows(key, part):
    return key_field(key).astype(jnp.bfloat16)


def draw_queries(key, part):
    query_key = jax.random.fold_in(key, 12)
    base = jax.random.truncated_normal(query_key, -4.5, 4.5, (TOKENS, KV_HEADS, QH, HD), jnp.float32)
    return base.reshape(TOKENS, KV_HEADS * QH * HD).astype(jnp.bfloat16)


def pass_counts(key):
    count_key, hit_key, pick_key = jax.random.split(jax.random.fold_in(key, 7), 3)
    counts = jax.random.randint(count_key, (TRACES,), PASSK, NMAX + 1, dtype=jnp.int32)
    chosen = jax.random.randint(pick_key, (), 0, TRACES, dtype=jnp.int32)
    slots = jnp.arange(TRACES, dtype=jnp.int32)
    counts = jnp.where(slots == chosen, NMAX, counts)
    hit_counts = jax.random.randint(hit_key, (TRACES,), 0, counts + 1, dtype=jnp.int32)
    hit_counts = jnp.where(slots == chosen, counts, hit_counts)
    hit_counts = jnp.where(slots == (chosen + 1) % TRACES, 0, hit_counts)
    return (counts, hit_counts)


def draw_group_size(key, part):
    return pass_counts(key)[0]


def draw_correct(key, part):
    return pass_counts(key)[1]


def block_levels(rng, shape, cuts, least, largest):
    level, own = 1.0, jax.random.fold_in(rng, 6)
    for axis_at, shards_of in cuts:
        heights = jnp.exp(jax.random.uniform(jax.random.fold_in(own, axis_at), (shards_of,), jnp.float32, least / len(cuts), largest / len(cuts)))
        level = level * jnp.repeat(heights, shape[axis_at] // shards_of).reshape([-1 if axis == axis_at else 1 for axis in range(len(shape))])
    return level


def profile(count, total, most, skew):
    portions = [(1 << 20) // math.isqrt(rank ** skew) + 1 for rank in range(2, count + 1)]
    surplus, given = total - most - (count - 1), [1] * (count - 1)
    while surplus > 0:
        movable = [i for i in range(count - 1) if given[i] < most]
        mass, left = sum([portions[i] for i in movable]), surplus
        for i in movable:
            addition = min(most - given[i], max(1, left * portions[i] // mass), surplus)
            given[i] = given[i] + addition
            surplus = surplus - addition
    return np.array([most] + given)


def uneven_parts(own_key, count, total, limit, slope):
    if count == 2:
        one = jax.random.randint(own_key, (), max(1, total - limit), min(limit, total - 1) + 1)
        return jnp.stack([one, total - one])
    tallies = jnp.asarray(profile(count, total, limit, slope), jnp.int32)
    twos = (count - 1) // 2
    donor, sink = tallies[1:1 + 2 * twos:2], tallies[2:2 + 2 * twos:2]
    room = jnp.minimum(donor - 1, limit - sink)
    passed = jax.random.randint(jax.random.fold_in(own_key, 1), (twos,), 0, 1 << 20) % (room + 1)
    tallies = tallies.at[1:1 + 2 * twos:2].set(donor - passed).at[2:2 + 2 * twos:2].set(sink + passed)
    return tallies[jax.random.permutation(jax.random.fold_in(own_key, 2), count)]


def gaussian(stream_key, dims, scale, reach, shards=(), held_as=jnp.bfloat16):
    level = block_levels(stream_key, dims, shards, -0.22, 0.18) if shards else 1.0
    drawn = jax.random.normal(stream_key, dims, jnp.float32) * scale * level
    return jnp.minimum(jnp.maximum(drawn, -reach), reach).astype(held_as)


def setup_inputs(seed: int = 0) -> dict:
    key_of = jax.random.split(jax.random.key(seed), 8)
    queries = draw_queries(jax.random.fold_in(key_of[7], 71), 0)
    key_rows = draw_key_rows(jax.random.fold_in(key_of[7], 71), 0)
    value_rows = gaussian(key_of[2], (TOKENS, KV_HEADS * HD), 3.0, 18.0, ((0, 16), (1, 2)))
    cotangent = gaussian(key_of[3], (TOKENS, KV_HEADS * QH * HD), 1.0, 6.0, ((0, 16), (1, 2)))
    trace_ids = jnp.searchsorted(jnp.cumsum(uneven_parts(key_of[4], TRACES, TOKENS, TOKENS // 4, 1)), jnp.arange(TOKENS), side="right").astype(jnp.int32)
    correct = draw_correct(jax.random.fold_in(key_of[7], 71), 0)
    group_size = draw_group_size(jax.random.fold_in(key_of[7], 71), 0)
    return dict(queries=queries, key_rows=key_rows, value_rows=value_rows, cotangent=cotangent, trace_ids=trace_ids, correct=correct, group_size=group_size)


def pass_rate(correct, group_size):
    counts = group_size.astype(jnp.float32)
    hit_counts = correct.astype(jnp.float32)
    product = jnp.ones_like(counts)
    for offset in range(PASSK):
        product = product * (counts - hit_counts - offset) / (counts - offset)
    return 1.0 - product

def reference(queries, key_rows, value_rows, cotangent, trace_ids, correct, group_size):
    pass_rates = pass_rate(correct, group_size)
    weights = pass_rates[trace_ids]
    out_grads = (weights[:, None] * cotangent.astype(jnp.float32)).astype(jnp.bfloat16)
    score_scale = 1.0 / math.sqrt(HD)
    query_heads = jnp.transpose(queries.reshape(TOKENS, KV_HEADS, QH, HD), (1, 0, 2, 3))
    grad_heads = jnp.transpose(out_grads.reshape(TOKENS, KV_HEADS, QH, HD), (1, 0, 2, 3))
    key_heads = jnp.transpose(key_rows.reshape(TOKENS, KV_HEADS, HD), (1, 0, 2))
    value_heads = jnp.transpose(value_rows.reshape(TOKENS, KV_HEADS, HD), (1, 0, 2))
    block_rows = math.gcd(TOKENS, 512)

    def one_head(operands):
        query_one, grad_one, key_one, value_one = operands
        grad_keys = jnp.zeros((TOKENS, HD), jnp.float32)
        grad_values = jnp.zeros((TOKENS, HD), jnp.float32)
        norms_list = []
        grads_list = []
        for step_index in range(TOKENS // block_rows):
            row_begin = step_index * block_rows
            row_end = row_begin + block_rows
            query_part = query_one[row_begin:row_end].astype(jnp.float32)
            grad_part = grad_one[row_begin:row_end].astype(jnp.float32)
            key_part = key_one[:row_end].astype(jnp.float32)
            value_part = value_one[:row_end].astype(jnp.float32)
            scores = jnp.einsum('tqd,kd->tqk', query_part, key_part) * score_scale
            key_pos = jnp.arange(row_end, dtype=jnp.int32)
            query_pos = row_begin + jnp.arange(block_rows, dtype=jnp.int32)
            visible = key_pos[None, None, :] <= query_pos[:, None, None]
            row_peak = lax.optimization_barrier(jnp.max(jnp.where(visible, scores, -1e+30), axis=2))
            exp_terms = jnp.where(visible, jnp.exp(scores - row_peak[:, :, None]), 0.0)
            log_norm = row_peak + jnp.log(lax.optimization_barrier(jnp.sum(exp_terms, axis=2)))
            probabilities = jnp.where(visible, jnp.exp(scores - log_norm[:, :, None]), 0.0)
            prob_bf16 = lax.optimization_barrier(probabilities.astype(jnp.bfloat16))
            grad_probs = jnp.einsum('tqd,kd->tqk', grad_part, value_part)
            delta_rows = lax.optimization_barrier(jnp.sum(probabilities * grad_probs, axis=2))
            grad_scores = (probabilities * (grad_probs - delta_rows[:, :, None])).astype(jnp.bfloat16)
            grad_scores = lax.optimization_barrier(grad_scores).astype(jnp.float32)
            grads_list.append(jnp.einsum('tqk,kd->tqd', grad_scores, key_part) * score_scale)
            grad_keys = grad_keys.at[:row_end].add(jnp.einsum('tqk,tqd->kd', grad_scores, query_part) * score_scale)
            grad_values = grad_values.at[:row_end].add(jnp.einsum('tqk,tqd->kd', prob_bf16.astype(jnp.float32), grad_part))
            norms_list.append(log_norm)
        return (jnp.concatenate(norms_list, 0), jnp.concatenate(grads_list, 0), grad_keys, grad_values)
    norms, grads, grad_keys, grad_values = lax.map(one_head, (query_heads, grad_heads, key_heads, value_heads))
    log_totals = jnp.transpose(norms, (1, 0, 2)).reshape(TOKENS, KV_HEADS * QH)
    grad_queries = jnp.transpose(grads, (1, 0, 2, 3)).reshape(TOKENS, KV_HEADS * QH * HD)
    grad_keys = jnp.transpose(grad_keys, (1, 0, 2)).reshape(TOKENS, KV_HEADS * HD).astype(jnp.bfloat16)
    grad_values = jnp.transpose(grad_values, (1, 0, 2)).reshape(TOKENS, KV_HEADS * HD).astype(jnp.bfloat16)
    return (log_totals, grad_queries, grad_keys, grad_values)
```

```python
import math

import jax
import jax.numpy as jnp
from jax import lax
from jax.sharding import Mesh, PartitionSpec as P

PASSK = 4


def pass_rate(correct, group_size):
    counts = group_size.astype(jnp.float32)
    hit_counts = correct.astype(jnp.float32)
    product = jnp.ones_like(counts)
    for offset in range(PASSK):
        product = product * (counts - hit_counts - offset) / (counts - offset)
    return 1.0 - product


def body(queries, key_rows, value_rows, cotangent, trace_ids, correct, group_size):
    tok_rows = queries.shape[0]
    half_rows = tok_rows // 2
    row_width = queries.shape[1]
    head_dim = key_rows.shape[1]
    head_count = row_width // head_dim
    chip_count = lax.axis_size("chip")
    ctx_count = chip_count * 2
    core = lax.axis_index("core")
    my_index = lax.axis_index("chip") * 2 + core
    length = tok_rows * ctx_count
    score_scale = 1.0 / math.sqrt(head_dim)
    pass_rates = pass_rate(correct, group_size)
    traces = jnp.arange(pass_rates.shape[0], dtype=jnp.int32)
    weights = jnp.sum(
        jnp.where(trace_ids[:, None] == traces[None, :], pass_rates[None, :], 0.0), axis=1
    )
    out_grads = (weights[:, None] * cotangent.astype(jnp.float32)).astype(jnp.bfloat16)
    first_base = my_index * tok_rows
    second_base = first_base + half_rows
    local_pos = jnp.arange(half_rows, dtype=jnp.int32)
    positions = jnp.concatenate([first_base + local_pos, second_base + local_pos], 0)
    last_first = first_base + half_rows - 1
    last_second = second_base + half_rows - 1
    query_all = queries.reshape(tok_rows, head_count, head_dim)
    grad_all = out_grads.reshape(tok_rows, head_count, head_dim)

    def run_block(running, key_block, value_block, key_start, block_fn):
        need_first = (key_start <= last_first).astype(jnp.int32)
        need_second = (key_start <= last_second).astype(jnp.int32)
        branch_index = need_first + 2 * need_second

        def skip_block(values_in):
            return values_in

        def first_only(values_in):
            return block_fn((0, half_rows), values_in, key_block, value_block, key_start)

        def second_only(values_in):
            return block_fn((half_rows, tok_rows), values_in, key_block, value_block, key_start)

        def both_halves(values_in):
            return block_fn((0, tok_rows), values_in, key_block, value_block, key_start)

        return lax.switch(branch_index, [skip_block, first_only, second_only, both_halves], running)

    def forward_block(row_span, running, key_block, value_block, key_start):
        row_begin, row_end = row_span
        row_peak, row_total, weighted = running
        query_part = query_all[row_begin:row_end]
        grad_part = grad_all[row_begin:row_end]
        query_pos = positions[row_begin:row_end]
        scores = (
            jnp.einsum("tqd,kd->tqk", query_part, key_block, preferred_element_type=jnp.float32)
            * score_scale
        )
        key_pos = key_start + jnp.arange(key_block.shape[0], dtype=jnp.int32)
        visible = key_pos[None, None, :] <= query_pos[:, None, None]
        block_peak = jnp.max(jnp.where(visible, scores, -1e30), axis=2)
        old_peak = row_peak[row_begin:row_end]
        new_peak = jnp.maximum(old_peak, block_peak)
        exp_terms = jnp.where(visible, jnp.exp(scores - new_peak[:, :, None]), 0.0)
        grad_probs = jnp.einsum(
            "tqd,kd->tqk", grad_part, value_block, preferred_element_type=jnp.float32
        )
        shrink = jnp.exp(old_peak - new_peak)
        new_total = row_total[row_begin:row_end] * shrink + jnp.sum(exp_terms, axis=2)
        new_weighted = weighted[row_begin:row_end] * shrink + jnp.sum(
            exp_terms * grad_probs, axis=2
        )
        return (
            row_peak.at[row_begin:row_end].set(new_peak),
            row_total.at[row_begin:row_end].set(new_total),
            weighted.at[row_begin:row_end].set(new_weighted),
        )

    row_peak = jnp.full((tok_rows, head_count), -1e30, jnp.float32)
    row_total = jnp.zeros((tok_rows, head_count), jnp.float32)
    weighted = jnp.zeros((tok_rows, head_count), jnp.float32)
    joined = jnp.concatenate([key_rows, value_rows], 1)
    spread = jnp.broadcast_to(joined[None], (ctx_count,) + joined.shape)
    gathered = lax.all_to_all(spread, ("chip", "core"), 0, 0, tiled=True).reshape(length, 2 * head_dim)
    key_piece = gathered[:, :head_dim]
    value_piece = gathered[:, head_dim:]
    piece_rows = key_piece.shape[0]
    block_rows = math.gcd(piece_rows, 512)

    def forward_step(step_index, statistics):
        offset = step_index * block_rows
        key_block = lax.dynamic_slice_in_dim(key_piece, offset, block_rows, 0)
        value_block = lax.dynamic_slice_in_dim(value_piece, offset, block_rows, 0)
        return run_block(statistics, key_block, value_block, offset, forward_block)

    statistics = lax.fori_loop(
        0, piece_rows // block_rows, forward_step, (row_peak, row_total, weighted)
    )
    folded = statistics + (key_piece, value_piece)
    row_peak, row_total, weighted, key_store, value_store = folded
    log_totals = row_peak + jnp.log(row_total)
    delta_rows = weighted / row_total

    def backward_block(row_span, running, key_block, value_block, key_start):
        row_begin, row_end = row_span
        grad_query, zero_block = running
        query_part = query_all[row_begin:row_end]
        grad_part = grad_all[row_begin:row_end]
        query_pos = positions[row_begin:row_end]
        scores = (
            jnp.einsum("tqd,kd->tqk", query_part, key_block, preferred_element_type=jnp.float32)
            * score_scale
        )
        key_pos = key_start + jnp.arange(key_block.shape[0], dtype=jnp.int32)
        visible = key_pos[None, None, :] <= query_pos[:, None, None]
        probabilities = jnp.where(
            visible, jnp.exp(scores - log_totals[row_begin:row_end][:, :, None]), 0.0
        )
        prob_bf16 = probabilities.astype(jnp.bfloat16)
        grad_probs = jnp.einsum(
            "tqd,kd->tqk", grad_part, value_block, preferred_element_type=jnp.float32
        )
        grad_scores = (
            probabilities * (grad_probs - delta_rows[row_begin:row_end][:, :, None])
        ).astype(jnp.bfloat16)
        query_add = (
            jnp.einsum("tqk,kd->tqd", grad_scores, key_block, preferred_element_type=jnp.float32)
            * score_scale
        )
        key_add = (
            jnp.einsum("tqk,tqd->kd", grad_scores, query_part, preferred_element_type=jnp.float32)
            * score_scale
        )
        value_add = jnp.einsum(
            "tqk,tqd->kd", prob_bf16, grad_part, preferred_element_type=jnp.float32
        )
        return (
            grad_query.at[row_begin:row_end].add(query_add),
            jnp.concatenate([key_add, value_add], 1),
        )

    query_zero = jnp.zeros((tok_rows, head_count, head_dim), jnp.float32)
    key_block_rows = math.gcd(length, 512)

    def backward_step(step_index, running):
        grad_query, partial_sums = running
        key_start = step_index * key_block_rows
        key_block = lax.dynamic_slice_in_dim(key_store, key_start, key_block_rows, 0)
        value_block = lax.dynamic_slice_in_dim(value_store, key_start, key_block_rows, 0)
        zero_block = jnp.zeros((key_block_rows, 2 * head_dim), jnp.float32)
        grad_query, block_sums = run_block(
            (grad_query, zero_block), key_block, value_block, key_start, backward_block
        )
        partial_sums = lax.dynamic_update_slice_in_dim(partial_sums, block_sums, key_start, 0)
        return (grad_query, partial_sums)

    grad_query, partial_sums = lax.fori_loop(
        0,
        length // key_block_rows,
        backward_step,
        (query_zero, jnp.zeros((length, 2 * head_dim), jnp.float32)),
    )
    chip_rows = 2 * tok_rows
    chip_sums = partial_sums.reshape(chip_count, chip_rows, 2 * head_dim)
    key_part = chip_sums[:, :, :head_dim]
    value_part = chip_sums[:, :, head_dim:]
    lead = core == 0
    swapped = lax.ppermute(jnp.where(lead, value_part, key_part), "core", [(0, 1), (1, 0)])
    own_part = jnp.where(lead, key_part, value_part) + swapped
    reduced = jnp.sum(lax.all_to_all(own_part, "chip", 0, 0, tiled=True), axis=0).astype(jnp.bfloat16)
    other = lax.ppermute(
        jnp.where(lead, reduced[tok_rows:], reduced[:tok_rows]), "core", [(0, 1), (1, 0)]
    )
    grad_keys = jnp.where(lead, reduced[:tok_rows], other)
    grad_values = jnp.where(lead, other, reduced[tok_rows:])
    query_grads = grad_query.reshape(tok_rows, row_width)
    return (log_totals, query_grads, grad_keys, grad_values)


def solution(mesh):
    order = [mesh.axis_names.index("ctx"), mesh.axis_names.index("head")]
    devices = mesh.devices.transpose(order)
    ctx_size, head_size = devices.shape
    chip_mesh = Mesh(devices.reshape(ctx_size // 2, 2, head_size), ("chip", "core", "head"))
    rows = P(("chip", "core"), "head")
    return jax.shard_map(
        body,
        mesh=chip_mesh,
        in_specs=(rows, rows, rows, rows, P(("chip", "core")), P(), P()),
        out_specs=(rows, rows, rows, rows),
        check_vma=False,
    )
```

```python
import functools
import math

import jax
import jax.numpy as jnp
from jax import lax
from jax.experimental import pallas as pl
from jax.experimental.pallas import tpu as pltpu
from jax.sharding import Mesh, PartitionSpec as P

PASSK = 4


def pass_rate(correct, group_size):
    counts = group_size.astype(jnp.float32)
    hit_counts = correct.astype(jnp.float32)
    product = jnp.ones_like(counts)
    for offset in range(PASSK):
        product = product * (counts - hit_counts - offset) / (counts - offset)
    return 1.0 - product


def attention_kernel(
    index_ref, query_ref, grad_ref, key_ref, value_ref,
    lse_ref, dq_ref, dk_ref, dv_ref, *, heads, head_dim, tok_rows, score_scale,
):
    index = index_ref[0]
    block_count = key_ref.shape[0] // tok_rows
    rows = heads * tok_rows
    queries = jnp.concatenate(
        [query_ref[:, h * head_dim:(h + 1) * head_dim] for h in range(heads)], 0
    )
    grads = jnp.concatenate(
        [grad_ref[:, h * head_dim:(h + 1) * head_dim] for h in range(heads)], 0
    )
    row_tok = lax.broadcasted_iota(jnp.int32, (heads, tok_rows, tok_rows), 1).reshape(rows, tok_rows)
    col_tok = lax.broadcasted_iota(jnp.int32, (rows, tok_rows), 1)
    visible = col_tok <= row_tok
    contract_last = (((1,), (1,)), ((), ()))
    contract_first = (((0,), (0,)), ((), ()))

    def scores_of(start):
        key_block = key_ref[pl.ds(start, tok_rows), :]
        scores = lax.dot_general(queries, key_block, contract_last, preferred_element_type=jnp.float32)
        return key_block, scores * score_scale

    def grad_probs_of(start):
        value_block = value_ref[pl.ds(start, tok_rows), :]
        return lax.dot_general(grads, value_block, contract_last, preferred_element_type=jnp.float32)

    def forward(block, carry, masked):
        peak, total, weighted = carry
        start = pl.multiple_of(block * tok_rows, tok_rows)
        _, scores = scores_of(start)
        if masked:
            scores = jnp.where(visible, scores, -1e30)
        grad_probs = grad_probs_of(start)
        new_peak = jnp.maximum(peak, jnp.max(scores, axis=1, keepdims=True))
        exp_terms = jnp.exp(scores - new_peak)
        if masked:
            exp_terms = jnp.where(visible, exp_terms, 0.0)
        shrink = jnp.exp(peak - new_peak)
        total = total * shrink + jnp.sum(exp_terms, axis=1, keepdims=True)
        weighted = weighted * shrink + jnp.sum(exp_terms * grad_probs, axis=1, keepdims=True)
        return new_peak, total, weighted

    start_carry = (
        jnp.full((rows, 1), -1e30, jnp.float32),
        jnp.zeros((rows, 1), jnp.float32),
        jnp.zeros((rows, 1), jnp.float32),
    )
    carry = lax.fori_loop(0, index, lambda b, c: forward(b, c, False), start_carry)
    peak, total, weighted = forward(index, carry, True)
    log_totals = peak + jnp.log(total)
    delta_rows = weighted / total
    lse_ref[...] = log_totals

    def backward(block, grad_query, masked):
        start = pl.multiple_of(block * tok_rows, tok_rows)
        key_block, scores = scores_of(start)
        probabilities = jnp.exp(scores - log_totals)
        if masked:
            probabilities = jnp.where(visible, probabilities, 0.0)
        grad_probs = grad_probs_of(start)
        grad_scores = (probabilities * (grad_probs - delta_rows)).astype(jnp.bfloat16)
        prob_bf16 = probabilities.astype(jnp.bfloat16)
        grad_query = grad_query + jnp.dot(grad_scores, key_block, preferred_element_type=jnp.float32)
        key_add = lax.dot_general(grad_scores, queries, contract_first, preferred_element_type=jnp.float32)
        value_add = lax.dot_general(prob_bf16, grads, contract_first, preferred_element_type=jnp.float32)
        dk_ref[pl.ds(start, tok_rows), :] = key_add * score_scale
        dv_ref[pl.ds(start, tok_rows), :] = value_add
        return grad_query

    grad_query = lax.fori_loop(
        0, index, lambda b, g: backward(b, g, False), jnp.zeros((rows, head_dim), jnp.float32)
    )
    grad_query = backward(index, grad_query, True) * score_scale
    for h in range(heads):
        dq_ref[:, h * head_dim:(h + 1) * head_dim] = grad_query[h * tok_rows:(h + 1) * tok_rows]

    def clear(block, unused):
        start = pl.multiple_of(block * tok_rows, tok_rows)
        dk_ref[pl.ds(start, tok_rows), :] = jnp.zeros((tok_rows, head_dim), jnp.float32)
        dv_ref[pl.ds(start, tok_rows), :] = jnp.zeros((tok_rows, head_dim), jnp.float32)
        return unused

    lax.fori_loop(index + 1, block_count, clear, 0)


def body(queries, key_rows, value_rows, cotangent, trace_ids, correct, group_size):
    tok_rows = queries.shape[0]
    row_width = queries.shape[1]
    head_dim = key_rows.shape[1]
    head_count = row_width // head_dim
    chip_count = lax.axis_size("chip")
    ctx_count = chip_count * 2
    core = lax.axis_index("core")
    my_index = lax.axis_index("chip") * 2 + core
    length = tok_rows * ctx_count
    score_scale = 1.0 / math.sqrt(head_dim)
    pass_rates = pass_rate(correct, group_size)
    traces = jnp.arange(pass_rates.shape[0], dtype=jnp.int32)
    weights = jnp.sum(
        jnp.where(trace_ids[:, None] == traces[None, :], pass_rates[None, :], 0.0), axis=1
    )
    out_grads = (weights[:, None] * cotangent.astype(jnp.float32)).astype(jnp.bfloat16)

    joined = jnp.concatenate([key_rows, value_rows], 1)
    spread = jnp.broadcast_to(joined[None], (ctx_count,) + joined.shape)
    gathered = lax.all_to_all(spread, ("chip", "core"), 0, 0, tiled=True).reshape(length, 2 * head_dim)
    key_piece = gathered[:, :head_dim]
    value_piece = gathered[:, head_dim:]

    rows = head_count * tok_rows
    vmem = pl.BlockSpec(memory_space=pltpu.MemorySpace.VMEM)
    smem = pl.BlockSpec(memory_space=pltpu.MemorySpace.SMEM)
    kernel = functools.partial(
        attention_kernel, heads=head_count, head_dim=head_dim, tok_rows=tok_rows, score_scale=score_scale
    )
    stacked_lse, query_grads, key_part, value_part = pl.pallas_call(
        kernel,
        out_shape=(
            jax.ShapeDtypeStruct((rows, 1), jnp.float32),
            jax.ShapeDtypeStruct((tok_rows, row_width), jnp.float32),
            jax.ShapeDtypeStruct((length, head_dim), jnp.float32),
            jax.ShapeDtypeStruct((length, head_dim), jnp.float32),
        ),
        in_specs=[smem, vmem, vmem, vmem, vmem],
        out_specs=(vmem, vmem, vmem, vmem),
    )(my_index.reshape(1).astype(jnp.int32), queries, out_grads, key_piece, value_piece)
    log_totals = stacked_lse.reshape(head_count, tok_rows).T

    chip_rows = 2 * tok_rows
    key_part = key_part.reshape(chip_count, chip_rows, head_dim)
    value_part = value_part.reshape(chip_count, chip_rows, head_dim)
    lead = core == 0
    swapped = lax.ppermute(jnp.where(lead, value_part, key_part), "core", [(0, 1), (1, 0)])
    own_part = jnp.where(lead, key_part, value_part) + swapped
    reduced = jnp.sum(lax.all_to_all(own_part, "chip", 0, 0, tiled=True), axis=0).astype(jnp.bfloat16)
    other = lax.ppermute(
        jnp.where(lead, reduced[tok_rows:], reduced[:tok_rows]), "core", [(0, 1), (1, 0)]
    )
    grad_keys = jnp.where(lead, reduced[:tok_rows], other)
    grad_values = jnp.where(lead, other, reduced[tok_rows:])
    return (log_totals, query_grads, grad_keys, grad_values)


def solution(mesh):
    order = [mesh.axis_names.index("ctx"), mesh.axis_names.index("head")]
    devices = mesh.devices.transpose(order)
    ctx_size, head_size = devices.shape
    chip_mesh = Mesh(devices.reshape(ctx_size // 2, 2, head_size), ("chip", "core", "head"))
    rows = P(("chip", "core"), "head")
    return jax.shard_map(
        body,
        mesh=chip_mesh,
        in_specs=(rows, rows, rows, rows, P(("chip", "core")), P(), P()),
        out_specs=(rows, rows, rows, rows),
        check_vma=False,
    )
```

```python
import functools
import math

import jax
import jax.numpy as jnp
from jax import lax
from jax.experimental import pallas as pl
from jax.experimental.pallas import tpu as pltpu
from jax.sharding import Mesh, PartitionSpec as P

PASSK = 4


def pass_rate(correct, group_size):
    counts = group_size.astype(jnp.float32)
    hit_counts = correct.astype(jnp.float32)
    product = jnp.ones_like(counts)
    for offset in range(PASSK):
        product = product * (counts - hit_counts - offset) / (counts - offset)
    return 1.0 - product


def attention_kernel(
    index_ref, query_ref, grad_ref, key_ref, value_ref,
    lse_ref, dq_ref, dk_ref, dv_ref, *, heads, head_dim, tok_rows, score_scale,
):
    index = index_ref[0]
    block_count = key_ref.shape[0] // tok_rows
    rows = heads * tok_rows
    queries = jnp.concatenate(
        [query_ref[:, h * head_dim:(h + 1) * head_dim] for h in range(heads)], 0
    )
    grads = jnp.concatenate(
        [grad_ref[:, h * head_dim:(h + 1) * head_dim] for h in range(heads)], 0
    )
    queries_t = queries.astype(jnp.float32).T.astype(jnp.bfloat16)
    grads_t = grads.astype(jnp.float32).T.astype(jnp.bfloat16)
    key_tok = lax.broadcasted_iota(jnp.int32, (tok_rows, rows), 0)
    row_tok = lax.rem(lax.broadcasted_iota(jnp.int32, (tok_rows, rows), 1), tok_rows)
    visible = key_tok <= row_tok
    contract_first = (((0,), (0,)), ((), ()))

    def blocks_of(block):
        start = pl.multiple_of(block * tok_rows, tok_rows)
        key_block = key_ref[pl.ds(start, tok_rows), :]
        value_block = value_ref[pl.ds(start, tok_rows), :]
        scores = jnp.dot(key_block, queries_t, preferred_element_type=jnp.float32) * score_scale
        grad_probs = jnp.dot(value_block, grads_t, preferred_element_type=jnp.float32)
        return start, key_block, scores, grad_probs

    def forward(block, carry, masked):
        peak, total, weighted = carry
        _, _, scores, grad_probs = blocks_of(block)
        if masked:
            scores = jnp.where(visible, scores, -1e30)
        new_peak = jnp.maximum(peak, jnp.max(scores, axis=0, keepdims=True))
        exp_terms = jnp.exp(scores - new_peak)
        if masked:
            exp_terms = jnp.where(visible, exp_terms, 0.0)
        shrink = jnp.exp(peak - new_peak)
        total = total * shrink + jnp.sum(exp_terms, axis=0, keepdims=True)
        weighted = weighted * shrink + jnp.sum(exp_terms * grad_probs, axis=0, keepdims=True)
        return new_peak, total, weighted

    start_carry = (
        jnp.full((1, rows), -1e30, jnp.float32),
        jnp.zeros((1, rows), jnp.float32),
        jnp.zeros((1, rows), jnp.float32),
    )
    carry = lax.fori_loop(0, index, lambda b, c: forward(b, c, False), start_carry)
    peak, total, weighted = forward(index, carry, True)
    log_totals = peak + jnp.log(total)
    delta_rows = weighted / total
    lse_ref[...] = log_totals

    def backward(block, grad_query_t, masked):
        start, key_block, scores, grad_probs = blocks_of(block)
        probabilities = jnp.exp(scores - log_totals)
        if masked:
            probabilities = jnp.where(visible, probabilities, 0.0)
        grad_scores = (probabilities * (grad_probs - delta_rows)).astype(jnp.bfloat16)
        prob_bf16 = probabilities.astype(jnp.bfloat16)
        grad_query_t = grad_query_t + lax.dot_general(
            key_block, grad_scores, contract_first, preferred_element_type=jnp.float32
        )
        key_add = jnp.dot(grad_scores, queries, preferred_element_type=jnp.float32)
        value_add = jnp.dot(prob_bf16, grads, preferred_element_type=jnp.float32)
        dk_ref[pl.ds(start, tok_rows), :] = key_add * score_scale
        dv_ref[pl.ds(start, tok_rows), :] = value_add
        return grad_query_t

    grad_query_t = lax.fori_loop(
        0, index, lambda b, g: backward(b, g, False), jnp.zeros((head_dim, rows), jnp.float32)
    )
    grad_query = (backward(index, grad_query_t, True) * score_scale).T
    for h in range(heads):
        dq_ref[:, h * head_dim:(h + 1) * head_dim] = grad_query[h * tok_rows:(h + 1) * tok_rows]

    def clear(block, unused):
        start = pl.multiple_of(block * tok_rows, tok_rows)
        dk_ref[pl.ds(start, tok_rows), :] = jnp.zeros((tok_rows, head_dim), jnp.float32)
        dv_ref[pl.ds(start, tok_rows), :] = jnp.zeros((tok_rows, head_dim), jnp.float32)
        return unused

    lax.fori_loop(index + 1, block_count, clear, 0)


def body(queries, key_rows, value_rows, cotangent, trace_ids, correct, group_size):
    tok_rows = queries.shape[0]
    row_width = queries.shape[1]
    head_dim = key_rows.shape[1]
    head_count = row_width // head_dim
    chip_count = lax.axis_size("chip")
    ctx_count = chip_count * 2
    core = lax.axis_index("core")
    my_index = lax.axis_index("chip") * 2 + core
    length = tok_rows * ctx_count
    score_scale = 1.0 / math.sqrt(head_dim)
    pass_rates = pass_rate(correct, group_size)
    traces = jnp.arange(pass_rates.shape[0], dtype=jnp.int32)
    weights = jnp.sum(
        jnp.where(trace_ids[:, None] == traces[None, :], pass_rates[None, :], 0.0), axis=1
    )
    out_grads = (weights[:, None] * cotangent.astype(jnp.float32)).astype(jnp.bfloat16)

    joined = jnp.concatenate([key_rows, value_rows], 1)
    spread = jnp.broadcast_to(joined[None], (ctx_count,) + joined.shape)
    gathered = lax.all_to_all(spread, ("chip", "core"), 0, 0, tiled=True).reshape(length, 2 * head_dim)
    key_piece = gathered[:, :head_dim]
    value_piece = gathered[:, head_dim:]

    rows = head_count * tok_rows
    vmem = pl.BlockSpec(memory_space=pltpu.MemorySpace.VMEM)
    smem = pl.BlockSpec(memory_space=pltpu.MemorySpace.SMEM)
    kernel = functools.partial(
        attention_kernel, heads=head_count, head_dim=head_dim, tok_rows=tok_rows, score_scale=score_scale
    )
    stacked_lse, query_grads, key_part, value_part = pl.pallas_call(
        kernel,
        out_shape=(
            jax.ShapeDtypeStruct((1, rows), jnp.float32),
            jax.ShapeDtypeStruct((tok_rows, row_width), jnp.float32),
            jax.ShapeDtypeStruct((length, head_dim), jnp.float32),
            jax.ShapeDtypeStruct((length, head_dim), jnp.float32),
        ),
        in_specs=[smem, vmem, vmem, vmem, vmem],
        out_specs=(vmem, vmem, vmem, vmem),
    )(my_index.reshape(1).astype(jnp.int32), queries, out_grads, key_piece, value_piece)
    log_totals = stacked_lse.reshape(head_count, tok_rows).T

    chip_rows = 2 * tok_rows
    key_part = key_part.reshape(chip_count, chip_rows, head_dim)
    value_part = value_part.reshape(chip_count, chip_rows, head_dim)
    lead = core == 0
    swapped = lax.ppermute(jnp.where(lead, value_part, key_part), "core", [(0, 1), (1, 0)])
    own_part = jnp.where(lead, key_part, value_part) + swapped
    reduced = jnp.sum(lax.all_to_all(own_part, "chip", 0, 0, tiled=True), axis=0).astype(jnp.bfloat16)
    other = lax.ppermute(
        jnp.where(lead, reduced[tok_rows:], reduced[:tok_rows]), "core", [(0, 1), (1, 0)]
    )
    grad_keys = jnp.where(lead, reduced[:tok_rows], other)
    grad_values = jnp.where(lead, other, reduced[tok_rows:])
    return (log_totals, query_grads, grad_keys, grad_values)


def solution(mesh):
    order = [mesh.axis_names.index("ctx"), mesh.axis_names.index("head")]
    devices = mesh.devices.transpose(order)
    ctx_size, head_size = devices.shape
    chip_mesh = Mesh(devices.reshape(ctx_size // 2, 2, head_size), ("chip", "core", "head"))
    rows = P(("chip", "core"), "head")
    return jax.shard_map(
        body,
        mesh=chip_mesh,
        in_specs=(rows, rows, rows, rows, P(("chip", "core")), P(), P()),
        out_specs=(rows, rows, rows, rows),
        check_vma=False,
    )
```

```python
import functools
import math

import jax
import jax.numpy as jnp
from jax import lax
from jax.experimental import pallas as pl
from jax.experimental.pallas import tpu as pltpu
from jax.sharding import Mesh, PartitionSpec as P

PASSK = 4


def pass_rate(correct, group_size):
    counts = group_size.astype(jnp.float32)
    hit_counts = correct.astype(jnp.float32)
    product = jnp.ones_like(counts)
    for offset in range(PASSK):
        product = product * (counts - hit_counts - offset) / (counts - offset)
    return 1.0 - product


def attention_kernel(
    index_ref, query_ref, grad_ref, joined_ref,
    lse_ref, dq_ref, keep_ref, send_ref, *, heads, head_dim, tok_rows, score_scale,
):
    index = index_ref[0]
    lead = index_ref[1] == 0
    block_count = joined_ref.shape[0] // tok_rows
    rows = heads * tok_rows
    queries = jnp.concatenate(
        [query_ref[:, h * head_dim:(h + 1) * head_dim] for h in range(heads)], 0
    )
    grads = jnp.concatenate(
        [grad_ref[:, h * head_dim:(h + 1) * head_dim] for h in range(heads)], 0
    )
    queries_t = queries.astype(jnp.float32).T.astype(jnp.bfloat16)
    grads_t = grads.astype(jnp.float32).T.astype(jnp.bfloat16)
    key_tok = lax.broadcasted_iota(jnp.int32, (tok_rows, rows), 0)
    row_tok = lax.rem(lax.broadcasted_iota(jnp.int32, (tok_rows, rows), 1), tok_rows)
    visible = key_tok <= row_tok
    contract_first = (((0,), (0,)), ((), ()))

    def blocks_of(block):
        start = pl.multiple_of(block * tok_rows, tok_rows)
        key_block = joined_ref[pl.ds(start, tok_rows), :head_dim]
        value_block = joined_ref[pl.ds(start, tok_rows), head_dim:]
        scores = jnp.dot(key_block, queries_t, preferred_element_type=jnp.float32) * score_scale
        grad_probs = jnp.dot(value_block, grads_t, preferred_element_type=jnp.float32)
        return start, key_block, scores, grad_probs

    def forward(block, carry, masked):
        peak, total, weighted = carry
        _, _, scores, grad_probs = blocks_of(block)
        if masked:
            scores = jnp.where(visible, scores, -1e30)
        new_peak = jnp.maximum(peak, jnp.max(scores, axis=0, keepdims=True))
        exp_terms = jnp.exp(scores - new_peak)
        if masked:
            exp_terms = jnp.where(visible, exp_terms, 0.0)
        shrink = jnp.exp(peak - new_peak)
        total = total * shrink + jnp.sum(exp_terms, axis=0, keepdims=True)
        weighted = weighted * shrink + jnp.sum(exp_terms * grad_probs, axis=0, keepdims=True)
        return new_peak, total, weighted

    start_carry = (
        jnp.full((1, rows), -1e30, jnp.float32),
        jnp.zeros((1, rows), jnp.float32),
        jnp.zeros((1, rows), jnp.float32),
    )
    carry = lax.fori_loop(0, index, lambda b, c: forward(b, c, False), start_carry)
    peak, total, weighted = forward(index, carry, True)
    log_totals = peak + jnp.log(total)
    delta_rows = weighted / total
    lse_ref[...] = log_totals

    def backward(block, grad_query_t, masked):
        start, key_block, scores, grad_probs = blocks_of(block)
        probabilities = jnp.exp(scores - log_totals)
        if masked:
            probabilities = jnp.where(visible, probabilities, 0.0)
        grad_scores = (probabilities * (grad_probs - delta_rows)).astype(jnp.bfloat16)
        prob_bf16 = probabilities.astype(jnp.bfloat16)
        grad_query_t = grad_query_t + lax.dot_general(
            key_block, grad_scores, contract_first, preferred_element_type=jnp.float32
        )
        key_add = jnp.dot(grad_scores, queries, preferred_element_type=jnp.float32)
        value_add = jnp.dot(prob_bf16, grads, preferred_element_type=jnp.float32)
        key_add = key_add * score_scale

        @pl.when(lead)
        def _():
            keep_ref[pl.ds(start, tok_rows), :] = key_add
            send_ref[pl.ds(start, tok_rows), :] = value_add

        @pl.when(jnp.logical_not(lead))
        def _():
            keep_ref[pl.ds(start, tok_rows), :] = value_add
            send_ref[pl.ds(start, tok_rows), :] = key_add

        return grad_query_t

    grad_query_t = lax.fori_loop(
        0, index, lambda b, g: backward(b, g, False), jnp.zeros((head_dim, rows), jnp.float32)
    )
    grad_query = (backward(index, grad_query_t, True) * score_scale).T
    for h in range(heads):
        dq_ref[:, h * head_dim:(h + 1) * head_dim] = grad_query[h * tok_rows:(h + 1) * tok_rows]

    def clear(block, unused):
        start = pl.multiple_of(block * tok_rows, tok_rows)
        keep_ref[pl.ds(start, tok_rows), :] = jnp.zeros((tok_rows, head_dim), jnp.float32)
        send_ref[pl.ds(start, tok_rows), :] = jnp.zeros((tok_rows, head_dim), jnp.float32)
        return unused

    lax.fori_loop(index + 1, block_count, clear, 0)


def body(queries, key_rows, value_rows, cotangent, trace_ids, correct, group_size):
    tok_rows = queries.shape[0]
    row_width = queries.shape[1]
    head_dim = key_rows.shape[1]
    head_count = row_width // head_dim
    chip_count = lax.axis_size("chip")
    ctx_count = chip_count * 2
    core = lax.axis_index("core")
    my_index = lax.axis_index("chip") * 2 + core
    length = tok_rows * ctx_count
    score_scale = 1.0 / math.sqrt(head_dim)
    pass_rates = pass_rate(correct, group_size)
    traces = jnp.arange(pass_rates.shape[0], dtype=jnp.int32)
    weights = jnp.sum(
        jnp.where(trace_ids[:, None] == traces[None, :], pass_rates[None, :], 0.0), axis=1
    )
    out_grads = (weights[:, None] * cotangent.astype(jnp.float32)).astype(jnp.bfloat16)

    joined = jnp.concatenate([key_rows, value_rows], 1)
    spread = jnp.broadcast_to(joined[None], (ctx_count,) + joined.shape)
    gathered = lax.all_to_all(spread, ("chip", "core"), 0, 0, tiled=True).reshape(length, 2 * head_dim)

    rows = head_count * tok_rows
    vmem = pl.BlockSpec(memory_space=pltpu.MemorySpace.VMEM)
    smem = pl.BlockSpec(memory_space=pltpu.MemorySpace.SMEM)
    kernel = functools.partial(
        attention_kernel, heads=head_count, head_dim=head_dim, tok_rows=tok_rows, score_scale=score_scale
    )
    stacked_lse, query_grads, keep_part, send_part = pl.pallas_call(
        kernel,
        out_shape=(
            jax.ShapeDtypeStruct((1, rows), jnp.float32),
            jax.ShapeDtypeStruct((tok_rows, row_width), jnp.float32),
            jax.ShapeDtypeStruct((length, head_dim), jnp.float32),
            jax.ShapeDtypeStruct((length, head_dim), jnp.float32),
        ),
        in_specs=[smem, vmem, vmem, vmem],
        out_specs=(vmem, vmem, vmem, vmem),
    )(jnp.stack([my_index, core]).astype(jnp.int32), queries, out_grads, gathered)
    log_totals = stacked_lse.reshape(head_count, tok_rows).T

    chip_rows = 2 * tok_rows
    keep_part = keep_part.reshape(chip_count, chip_rows, head_dim)
    send_part = send_part.reshape(chip_count, chip_rows, head_dim)
    lead = core == 0
    own_part = keep_part + lax.ppermute(send_part, "core", [(0, 1), (1, 0)])
    reduced = jnp.sum(lax.all_to_all(own_part, "chip", 0, 0, tiled=True), axis=0).astype(jnp.bfloat16)
    other = lax.ppermute(
        jnp.where(lead, reduced[tok_rows:], reduced[:tok_rows]), "core", [(0, 1), (1, 0)]
    )
    grad_keys = jnp.where(lead, reduced[:tok_rows], other)
    grad_values = jnp.where(lead, other, reduced[tok_rows:])
    return (log_totals, query_grads, grad_keys, grad_values)


def solution(mesh):
    order = [mesh.axis_names.index("ctx"), mesh.axis_names.index("head")]
    devices = mesh.devices.transpose(order)
    ctx_size, head_size = devices.shape
    chip_mesh = Mesh(devices.reshape(ctx_size // 2, 2, head_size), ("chip", "core", "head"))
    rows = P(("chip", "core"), "head")
    return jax.shard_map(
        body,
        mesh=chip_mesh,
        in_specs=(rows, rows, rows, rows, P(("chip", "core")), P(), P()),
        out_specs=(rows, rows, rows, rows),
        check_vma=False,
    )
```

```python
import functools
import math

import jax
import jax.numpy as jnp
from jax import lax
from jax.experimental import pallas as pl
from jax.experimental.pallas import tpu as pltpu
from jax.sharding import Mesh, PartitionSpec as P

PASSK = 4


def pass_rate(correct, group_size):
    counts = group_size.astype(jnp.float32)
    hit_counts = correct.astype(jnp.float32)
    product = jnp.ones_like(counts)
    for offset in range(PASSK):
        product = product * (counts - hit_counts - offset) / (counts - offset)
    return 1.0 - product


def attention_kernel(
    index_ref, query_ref, grad_ref, mine_ref, other_ref,
    lse_ref, dq_ref, dk_ref, dv_ref, *, heads, head_dim, tok_rows, score_scale,
):
    index = index_ref[0]
    core = index_ref[1]
    block_count = 2 * mine_ref.shape[0] // tok_rows
    rows = heads * tok_rows
    queries = jnp.concatenate(
        [query_ref[:, h * head_dim:(h + 1) * head_dim] for h in range(heads)], 0
    )
    grads = jnp.concatenate(
        [grad_ref[:, h * head_dim:(h + 1) * head_dim] for h in range(heads)], 0
    )
    queries_t = queries.astype(jnp.float32).T.astype(jnp.bfloat16)
    grads_t = grads.astype(jnp.float32).T.astype(jnp.bfloat16)
    key_tok = lax.broadcasted_iota(jnp.int32, (tok_rows, rows), 0)
    row_tok = lax.rem(lax.broadcasted_iota(jnp.int32, (tok_rows, rows), 1), tok_rows)
    visible = key_tok <= row_tok
    contract_first = (((0,), (0,)), ((), ()))

    def blocks_of(block):
        start = pl.multiple_of(block * tok_rows, tok_rows)
        source = pl.multiple_of((block // 2) * tok_rows, tok_rows)
        joined_block = jnp.where(
            block % 2 == core,
            mine_ref[pl.ds(source, tok_rows), :],
            other_ref[pl.ds(source, tok_rows), :],
        )
        key_block = joined_block[:, :head_dim]
        value_block = joined_block[:, head_dim:]
        scores = jnp.dot(key_block, queries_t, preferred_element_type=jnp.float32) * score_scale
        grad_probs = jnp.dot(value_block, grads_t, preferred_element_type=jnp.float32)
        return start, key_block, scores, grad_probs

    def forward(block, carry, masked):
        peak, total, weighted = carry
        _, _, scores, grad_probs = blocks_of(block)
        if masked:
            scores = jnp.where(visible, scores, -1e30)
        new_peak = jnp.maximum(peak, jnp.max(scores, axis=0, keepdims=True))
        exp_terms = jnp.exp(scores - new_peak)
        if masked:
            exp_terms = jnp.where(visible, exp_terms, 0.0)
        shrink = jnp.exp(peak - new_peak)
        total = total * shrink + jnp.sum(exp_terms, axis=0, keepdims=True)
        weighted = weighted * shrink + jnp.sum(exp_terms * grad_probs, axis=0, keepdims=True)
        return new_peak, total, weighted

    start_carry = (
        jnp.full((1, rows), -1e30, jnp.float32),
        jnp.zeros((1, rows), jnp.float32),
        jnp.zeros((1, rows), jnp.float32),
    )
    carry = lax.fori_loop(0, index, lambda b, c: forward(b, c, False), start_carry)
    peak, total, weighted = forward(index, carry, True)
    log_totals = peak + jnp.log(total)
    delta_rows = weighted / total
    lse_ref[...] = log_totals

    def backward(block, grad_query_t, masked):
        start, key_block, scores, grad_probs = blocks_of(block)
        probabilities = jnp.exp(scores - log_totals)
        if masked:
            probabilities = jnp.where(visible, probabilities, 0.0)
        grad_scores = (probabilities * (grad_probs - delta_rows)).astype(jnp.bfloat16)
        prob_bf16 = probabilities.astype(jnp.bfloat16)
        grad_query_t = grad_query_t + lax.dot_general(
            key_block, grad_scores, contract_first, preferred_element_type=jnp.float32
        )
        key_add = jnp.dot(grad_scores, queries, preferred_element_type=jnp.float32)
        value_add = jnp.dot(prob_bf16, grads, preferred_element_type=jnp.float32)
        dk_ref[pl.ds(start, tok_rows), :] = key_add * score_scale
        dv_ref[pl.ds(start, tok_rows), :] = value_add
        return grad_query_t

    grad_query_t = lax.fori_loop(
        0, index, lambda b, g: backward(b, g, False), jnp.zeros((head_dim, rows), jnp.float32)
    )
    grad_query = (backward(index, grad_query_t, True) * score_scale).T
    for h in range(heads):
        dq_ref[:, h * head_dim:(h + 1) * head_dim] = grad_query[h * tok_rows:(h + 1) * tok_rows]

    def clear(block, unused):
        start = pl.multiple_of(block * tok_rows, tok_rows)
        dk_ref[pl.ds(start, tok_rows), :] = jnp.zeros((tok_rows, head_dim), jnp.float32)
        dv_ref[pl.ds(start, tok_rows), :] = jnp.zeros((tok_rows, head_dim), jnp.float32)
        return unused

    lax.fori_loop(index + 1, block_count, clear, 0)


def body(queries, key_rows, value_rows, cotangent, trace_ids, correct, group_size):
    tok_rows = queries.shape[0]
    row_width = queries.shape[1]
    head_dim = key_rows.shape[1]
    head_count = row_width // head_dim
    chip_count = lax.axis_size("chip")
    ctx_count = chip_count * 2
    core = lax.axis_index("core")
    my_index = lax.axis_index("chip") * 2 + core
    length = tok_rows * ctx_count
    score_scale = 1.0 / math.sqrt(head_dim)
    pass_rates = pass_rate(correct, group_size)
    traces = jnp.arange(pass_rates.shape[0], dtype=jnp.int32)
    weights = jnp.sum(
        jnp.where(trace_ids[:, None] == traces[None, :], pass_rates[None, :], 0.0), axis=1
    )
    out_grads = (weights[:, None] * cotangent.astype(jnp.float32)).astype(jnp.bfloat16)

    joined = jnp.concatenate([key_rows, value_rows], 1)
    spread = jnp.broadcast_to(joined[None], (chip_count,) + joined.shape)
    mine = lax.all_to_all(spread, "chip", 0, 0, tiled=True)
    other = lax.ppermute(mine, "core", [(0, 1), (1, 0)])
    mine = mine.reshape(chip_count * tok_rows, 2 * head_dim)
    other = other.reshape(chip_count * tok_rows, 2 * head_dim)

    rows = head_count * tok_rows
    vmem = pl.BlockSpec(memory_space=pltpu.MemorySpace.VMEM)
    smem = pl.BlockSpec(memory_space=pltpu.MemorySpace.SMEM)
    kernel = functools.partial(
        attention_kernel, heads=head_count, head_dim=head_dim, tok_rows=tok_rows, score_scale=score_scale
    )
    stacked_lse, query_grads, key_part, value_part = pl.pallas_call(
        kernel,
        out_shape=(
            jax.ShapeDtypeStruct((1, rows), jnp.float32),
            jax.ShapeDtypeStruct((tok_rows, row_width), jnp.float32),
            jax.ShapeDtypeStruct((length, head_dim), jnp.float32),
            jax.ShapeDtypeStruct((length, head_dim), jnp.float32),
        ),
        in_specs=[smem, vmem, vmem, vmem, vmem],
        out_specs=(vmem, vmem, vmem, vmem),
    )(jnp.stack([my_index, core]).astype(jnp.int32), queries, out_grads, mine, other)
    log_totals = stacked_lse.reshape(head_count, tok_rows).T

    chip_rows = 2 * tok_rows
    key_part = key_part.reshape(chip_count, chip_rows, head_dim)
    value_part = value_part.reshape(chip_count, chip_rows, head_dim)
    lead = core == 0
    swapped = lax.ppermute(jnp.where(lead, value_part, key_part), "core", [(0, 1), (1, 0)])
    own_part = jnp.where(lead, key_part, value_part) + swapped
    reduced = jnp.sum(lax.all_to_all(own_part, "chip", 0, 0, tiled=True), axis=0).astype(jnp.bfloat16)
    other = lax.ppermute(
        jnp.where(lead, reduced[tok_rows:], reduced[:tok_rows]), "core", [(0, 1), (1, 0)]
    )
    grad_keys = jnp.where(lead, reduced[:tok_rows], other)
    grad_values = jnp.where(lead, other, reduced[tok_rows:])
    return (log_totals, query_grads, grad_keys, grad_values)


def solution(mesh):
    order = [mesh.axis_names.index("ctx"), mesh.axis_names.index("head")]
    devices = mesh.devices.transpose(order)
    ctx_size, head_size = devices.shape
    chip_mesh = Mesh(devices.reshape(ctx_size // 2, 2, head_size), ("chip", "core", "head"))
    rows = P(("chip", "core"), "head")
    return jax.shard_map(
        body,
        mesh=chip_mesh,
        in_specs=(rows, rows, rows, rows, P(("chip", "core")), P(), P()),
        out_specs=(rows, rows, rows, rows),
        check_vma=False,
    )
```

```python
import functools
import math

import jax
import jax.numpy as jnp
from jax import lax
from jax.experimental import pallas as pl
from jax.experimental.pallas import tpu as pltpu
from jax.sharding import Mesh, PartitionSpec as P

PASSK = 4


def pass_rate(correct, group_size):
    counts = group_size.astype(jnp.float32)
    hit_counts = correct.astype(jnp.float32)
    product = jnp.ones_like(counts)
    for offset in range(PASSK):
        product = product * (counts - hit_counts - offset) / (counts - offset)
    return 1.0 - product


def attention_kernel(
    index_ref, query_ref, grad_ref, mine_ref, other_ref,
    lse_ref, dq_ref, dk_ref, dv_ref, *, heads, head_dim, tok_rows, score_scale, tile_blocks,
):
    index = index_ref[0]
    core = index_ref[1]
    pair_rows = tile_blocks * tok_rows
    pair_count = mine_ref.shape[0] * 2 // pair_rows
    last = index // tile_blocks
    rows = heads * tok_rows
    queries = jnp.concatenate(
        [query_ref[:, h * head_dim:(h + 1) * head_dim] for h in range(heads)], 0
    )
    grads = jnp.concatenate(
        [grad_ref[:, h * head_dim:(h + 1) * head_dim] for h in range(heads)], 0
    )
    queries_t = queries.astype(jnp.float32).T.astype(jnp.bfloat16)
    grads_t = grads.astype(jnp.float32).T.astype(jnp.bfloat16)
    key_tok = lax.broadcasted_iota(jnp.int32, (pair_rows, rows), 0)
    row_tok = lax.rem(lax.broadcasted_iota(jnp.int32, (pair_rows, rows), 1), tok_rows)
    visible = key_tok <= row_tok + (index - tile_blocks * last) * tok_rows
    contract_first = (((0,), (0,)), ((), ()))
    lead = core == 0

    def blocks_of(pair):
        parts = []
        for chip in range(tile_blocks // 2):
            source = pl.multiple_of((pair * (tile_blocks // 2) + chip) * tok_rows, tok_rows)
            own = mine_ref[pl.ds(source, tok_rows), :]
            partner = other_ref[pl.ds(source, tok_rows), :]
            parts += [jnp.where(lead, own, partner), jnp.where(lead, partner, own)]
        joined = jnp.concatenate(parts, 0)
        key_block = joined[:, :head_dim]
        value_block = joined[:, head_dim:]
        scores = jnp.dot(key_block, queries_t, preferred_element_type=jnp.float32) * score_scale
        grad_probs = jnp.dot(value_block, grads_t, preferred_element_type=jnp.float32)
        return pl.multiple_of(pair * pair_rows, pair_rows), key_block, scores, grad_probs

    def forward(pair, carry, masked):
        peak, total, weighted = carry
        _, _, scores, grad_probs = blocks_of(pair)
        if masked:
            scores = jnp.where(visible, scores, -1e30)
        new_peak = jnp.maximum(peak, jnp.max(scores, axis=0, keepdims=True))
        exp_terms = jnp.exp(scores - new_peak)
        if masked:
            exp_terms = jnp.where(visible, exp_terms, 0.0)
        shrink = jnp.exp(peak - new_peak)
        total = total * shrink + jnp.sum(exp_terms, axis=0, keepdims=True)
        weighted = weighted * shrink + jnp.sum(exp_terms * grad_probs, axis=0, keepdims=True)
        return new_peak, total, weighted

    start_carry = (
        jnp.full((1, rows), -1e30, jnp.float32),
        jnp.zeros((1, rows), jnp.float32),
        jnp.zeros((1, rows), jnp.float32),
    )
    carry = lax.fori_loop(0, last, lambda b, c: forward(b, c, False), start_carry)
    peak, total, weighted = forward(last, carry, True)
    log_totals = peak + jnp.log(total)
    delta_rows = weighted / total
    lse_ref[...] = log_totals

    def backward(pair, grad_query_t, masked):
        start, key_block, scores, grad_probs = blocks_of(pair)
        probabilities = jnp.exp(scores - log_totals)
        if masked:
            probabilities = jnp.where(visible, probabilities, 0.0)
        grad_scores = (probabilities * (grad_probs - delta_rows)).astype(jnp.bfloat16)
        prob_bf16 = probabilities.astype(jnp.bfloat16)
        grad_query_t = grad_query_t + lax.dot_general(
            key_block, grad_scores, contract_first, preferred_element_type=jnp.float32
        )
        key_add = jnp.dot(grad_scores, queries, preferred_element_type=jnp.float32)
        value_add = jnp.dot(prob_bf16, grads, preferred_element_type=jnp.float32)
        dk_ref[pl.ds(start, pair_rows), :] = key_add * score_scale
        dv_ref[pl.ds(start, pair_rows), :] = value_add
        return grad_query_t

    grad_query_t = lax.fori_loop(
        0, last, lambda b, g: backward(b, g, False), jnp.zeros((head_dim, rows), jnp.float32)
    )
    grad_query = (backward(last, grad_query_t, True) * score_scale).T
    for h in range(heads):
        dq_ref[:, h * head_dim:(h + 1) * head_dim] = grad_query[h * tok_rows:(h + 1) * tok_rows]

    def clear(pair, unused):
        start = pl.multiple_of(pair * pair_rows, pair_rows)
        dk_ref[pl.ds(start, pair_rows), :] = jnp.zeros((pair_rows, head_dim), jnp.float32)
        dv_ref[pl.ds(start, pair_rows), :] = jnp.zeros((pair_rows, head_dim), jnp.float32)
        return unused

    lax.fori_loop(last + 1, pair_count, clear, 0)


def body(queries, key_rows, value_rows, cotangent, trace_ids, correct, group_size):
    tok_rows = queries.shape[0]
    row_width = queries.shape[1]
    head_dim = key_rows.shape[1]
    head_count = row_width // head_dim
    chip_count = lax.axis_size("chip")
    ctx_count = chip_count * 2
    core = lax.axis_index("core")
    my_index = lax.axis_index("chip") * 2 + core
    length = tok_rows * ctx_count
    score_scale = 1.0 / math.sqrt(head_dim)
    pass_rates = pass_rate(correct, group_size)
    traces = jnp.arange(pass_rates.shape[0], dtype=jnp.int32)
    weights = jnp.sum(
        jnp.where(trace_ids[:, None] == traces[None, :], pass_rates[None, :], 0.0), axis=1
    )
    out_grads = (weights[:, None] * cotangent.astype(jnp.float32)).astype(jnp.bfloat16)

    joined = jnp.concatenate([key_rows, value_rows], 1)
    spread = jnp.broadcast_to(joined[None], (chip_count,) + joined.shape)
    mine = lax.all_to_all(spread, "chip", 0, 0, tiled=True)
    other = lax.ppermute(mine, "core", [(0, 1), (1, 0)])
    mine = mine.reshape(chip_count * tok_rows, 2 * head_dim)
    other = other.reshape(chip_count * tok_rows, 2 * head_dim)

    rows = head_count * tok_rows
    vmem = pl.BlockSpec(memory_space=pltpu.MemorySpace.VMEM)
    smem = pl.BlockSpec(memory_space=pltpu.MemorySpace.SMEM)
    kernel = functools.partial(
        attention_kernel, heads=head_count, head_dim=head_dim, tok_rows=tok_rows,
        score_scale=score_scale, tile_blocks=math.gcd(ctx_count, 4),
    )
    stacked_lse, query_grads, key_part, value_part = pl.pallas_call(
        kernel,
        out_shape=(
            jax.ShapeDtypeStruct((1, rows), jnp.float32),
            jax.ShapeDtypeStruct((tok_rows, row_width), jnp.float32),
            jax.ShapeDtypeStruct((length, head_dim), jnp.float32),
            jax.ShapeDtypeStruct((length, head_dim), jnp.float32),
        ),
        in_specs=[smem, vmem, vmem, vmem, vmem],
        out_specs=(vmem, vmem, vmem, vmem),
    )(jnp.stack([my_index, core]).astype(jnp.int32), queries, out_grads, mine, other)
    log_totals = stacked_lse.reshape(head_count, tok_rows).T

    chip_rows = 2 * tok_rows
    key_part = key_part.reshape(chip_count, chip_rows, head_dim)
    value_part = value_part.reshape(chip_count, chip_rows, head_dim)
    lead = core == 0
    swapped = lax.ppermute(jnp.where(lead, value_part, key_part), "core", [(0, 1), (1, 0)])
    own_part = jnp.where(lead, key_part, value_part) + swapped
    reduced = jnp.sum(lax.all_to_all(own_part, "chip", 0, 0, tiled=True), axis=0).astype(jnp.bfloat16)
    other = lax.ppermute(
        jnp.where(lead, reduced[tok_rows:], reduced[:tok_rows]), "core", [(0, 1), (1, 0)]
    )
    grad_keys = jnp.where(lead, reduced[:tok_rows], other)
    grad_values = jnp.where(lead, other, reduced[tok_rows:])
    return (log_totals, query_grads, grad_keys, grad_values)


def solution(mesh):
    order = [mesh.axis_names.index("ctx"), mesh.axis_names.index("head")]
    devices = mesh.devices.transpose(order)
    ctx_size, head_size = devices.shape
    chip_mesh = Mesh(devices.reshape(ctx_size // 2, 2, head_size), ("chip", "core", "head"))
    rows = P(("chip", "core"), "head")
    return jax.shard_map(
        body,
        mesh=chip_mesh,
        in_specs=(rows, rows, rows, rows, P(("chip", "core")), P(), P()),
        out_specs=(rows, rows, rows, rows),
        check_vma=False,
    )
```

```python
import functools
import math

import jax
import jax.numpy as jnp
from jax import lax
from jax.experimental import pallas as pl
from jax.experimental.pallas import tpu as pltpu
from jax.sharding import Mesh, PartitionSpec as P

PASSK = 4


def pass_rate(correct, group_size):
    counts = group_size.astype(jnp.float32)
    hit_counts = correct.astype(jnp.float32)
    product = jnp.ones_like(counts)
    for offset in range(PASSK):
        product = product * (counts - hit_counts - offset) / (counts - offset)
    return 1.0 - product


def attention_kernel(
    index_ref, query_ref, grad_ref, mine_ref, other_ref,
    lse_ref, dq_ref, dk_ref, dv_ref, *, heads, head_dim, tok_rows, score_scale, tile_blocks,
):
    index = index_ref[0]
    core = index_ref[1]
    pair_rows = tile_blocks * tok_rows
    pair_count = mine_ref.shape[0] * 2 // pair_rows
    last = index // tile_blocks
    rows = heads * tok_rows
    queries = jnp.concatenate(
        [query_ref[:, h * head_dim:(h + 1) * head_dim] for h in range(heads)], 0
    )
    grads = jnp.concatenate(
        [grad_ref[:, h * head_dim:(h + 1) * head_dim] for h in range(heads)], 0
    )
    queries_t = queries.astype(jnp.float32).T.astype(jnp.bfloat16)
    grads_t = grads.astype(jnp.float32).T.astype(jnp.bfloat16)
    key_tok = lax.broadcasted_iota(jnp.int32, (pair_rows, rows), 0)
    row_tok = lax.rem(lax.broadcasted_iota(jnp.int32, (pair_rows, rows), 1), tok_rows)
    visible = key_tok <= row_tok + (index - tile_blocks * last) * tok_rows
    contract_first = (((0,), (0,)), ((), ()))
    lead = core == 0

    def blocks_of(pair):
        parts = []
        for chip in range(tile_blocks // 2):
            source = pl.multiple_of((pair * (tile_blocks // 2) + chip) * tok_rows, tok_rows)
            own = mine_ref[pl.ds(source, tok_rows), :]
            partner = other_ref[pl.ds(source, tok_rows), :]
            parts += [jnp.where(lead, own, partner), jnp.where(lead, partner, own)]
        joined = jnp.concatenate(parts, 0)
        key_block = joined[:, :head_dim]
        value_block = joined[:, head_dim:]
        scores = jnp.dot(key_block, queries_t, preferred_element_type=jnp.float32) * score_scale
        grad_probs = jnp.dot(value_block, grads_t, preferred_element_type=jnp.float32)
        return pl.multiple_of(pair * pair_rows, pair_rows), key_block, scores, grad_probs

    def forward(pair, carry, masked):
        peak, total, weighted = carry
        _, _, scores, grad_probs = blocks_of(pair)
        if masked:
            scores = jnp.where(visible, scores, -1e30)
        new_peak = jnp.maximum(peak, jnp.max(scores, axis=0, keepdims=True))
        exp_terms = jnp.exp(scores - new_peak)
        if masked:
            exp_terms = jnp.where(visible, exp_terms, 0.0)
        shrink = jnp.exp(peak - new_peak)
        total = total * shrink + jnp.sum(exp_terms, axis=0, keepdims=True)
        weighted = weighted * shrink + jnp.sum(exp_terms * grad_probs, axis=0, keepdims=True)
        return new_peak, total, weighted

    start_carry = (
        jnp.full((1, rows), -1e30, jnp.float32),
        jnp.zeros((1, rows), jnp.float32),
        jnp.zeros((1, rows), jnp.float32),
    )
    carry = lax.fori_loop(0, last, lambda b, c: forward(b, c, False), start_carry)
    peak, total, weighted = forward(last, carry, True)
    log_totals = peak + jnp.log(total)
    delta_rows = weighted / total
    lse_ref[...] = log_totals

    def backward(pair, grad_query_t, masked):
        start, key_block, scores, grad_probs = blocks_of(pair)
        probabilities = jnp.exp(scores - log_totals)
        if masked:
            probabilities = jnp.where(visible, probabilities, 0.0)
        grad_scores = (probabilities * (grad_probs - delta_rows)).astype(jnp.bfloat16)
        prob_bf16 = probabilities.astype(jnp.bfloat16)
        grad_query_t = grad_query_t + lax.dot_general(
            key_block, grad_scores, contract_first, preferred_element_type=jnp.float32
        )
        key_add = jnp.dot(grad_scores, queries, preferred_element_type=jnp.float32)
        value_add = jnp.dot(prob_bf16, grads, preferred_element_type=jnp.float32)
        dk_ref[pl.ds(start, pair_rows), :] = key_add * score_scale
        dv_ref[pl.ds(start, pair_rows), :] = value_add
        return grad_query_t

    grad_query_t = lax.fori_loop(
        0, last, lambda b, g: backward(b, g, False), jnp.zeros((head_dim, rows), jnp.float32)
    )
    grad_query = (backward(last, grad_query_t, True) * score_scale).T
    for h in range(heads):
        dq_ref[:, h * head_dim:(h + 1) * head_dim] = grad_query[h * tok_rows:(h + 1) * tok_rows]

    def clear(pair, unused):
        start = pl.multiple_of(pair * pair_rows, pair_rows)
        dk_ref[pl.ds(start, pair_rows), :] = jnp.zeros((pair_rows, head_dim), jnp.float32)
        dv_ref[pl.ds(start, pair_rows), :] = jnp.zeros((pair_rows, head_dim), jnp.float32)
        return unused

    lax.fori_loop(last + 1, pair_count, clear, 0)


def body(queries, key_rows, value_rows, cotangent, trace_ids, correct, group_size):
    tok_rows = queries.shape[0]
    row_width = queries.shape[1]
    head_dim = key_rows.shape[1]
    head_count = row_width // head_dim
    chip_count = lax.axis_size("chip")
    ctx_count = chip_count * 2
    core = lax.axis_index("core")
    my_index = lax.axis_index("chip") * 2 + core
    length = tok_rows * ctx_count
    score_scale = 1.0 / math.sqrt(head_dim)
    pass_rates = pass_rate(correct, group_size)
    traces = jnp.arange(pass_rates.shape[0], dtype=jnp.int32)
    weights = jnp.sum(
        jnp.where(trace_ids[:, None] == traces[None, :], pass_rates[None, :], 0.0), axis=1
    )
    out_grads = (weights[:, None] * cotangent.astype(jnp.float32)).astype(jnp.bfloat16)

    joined = jnp.concatenate([key_rows, value_rows], 1)
    spread = jnp.broadcast_to(joined[None], (chip_count,) + joined.shape)
    mine = lax.all_to_all(spread, "chip", 0, 0, tiled=True)
    other = lax.ppermute(mine, "core", [(0, 1), (1, 0)])
    mine = mine.reshape(chip_count * tok_rows, 2 * head_dim)
    other = other.reshape(chip_count * tok_rows, 2 * head_dim)

    rows = head_count * tok_rows
    vmem = pl.BlockSpec(memory_space=pltpu.MemorySpace.VMEM)
    smem = pl.BlockSpec(memory_space=pltpu.MemorySpace.SMEM)
    kernel = functools.partial(
        attention_kernel, heads=head_count, head_dim=head_dim, tok_rows=tok_rows,
        score_scale=score_scale, tile_blocks=math.gcd(ctx_count, 8),
    )
    stacked_lse, query_grads, key_part, value_part = pl.pallas_call(
        kernel,
        out_shape=(
            jax.ShapeDtypeStruct((1, rows), jnp.float32),
            jax.ShapeDtypeStruct((tok_rows, row_width), jnp.float32),
            jax.ShapeDtypeStruct((length, head_dim), jnp.float32),
            jax.ShapeDtypeStruct((length, head_dim), jnp.float32),
        ),
        in_specs=[smem, vmem, vmem, vmem, vmem],
        out_specs=(vmem, vmem, vmem, vmem),
    )(jnp.stack([my_index, core]).astype(jnp.int32), queries, out_grads, mine, other)
    log_totals = stacked_lse.reshape(head_count, tok_rows).T

    chip_rows = 2 * tok_rows
    key_part = key_part.reshape(chip_count, chip_rows, head_dim)
    value_part = value_part.reshape(chip_count, chip_rows, head_dim)
    lead = core == 0
    swapped = lax.ppermute(jnp.where(lead, value_part, key_part), "core", [(0, 1), (1, 0)])
    own_part = jnp.where(lead, key_part, value_part) + swapped
    reduced = jnp.sum(lax.all_to_all(own_part, "chip", 0, 0, tiled=True), axis=0).astype(jnp.bfloat16)
    other = lax.ppermute(
        jnp.where(lead, reduced[tok_rows:], reduced[:tok_rows]), "core", [(0, 1), (1, 0)]
    )
    grad_keys = jnp.where(lead, reduced[:tok_rows], other)
    grad_values = jnp.where(lead, other, reduced[tok_rows:])
    return (log_totals, query_grads, grad_keys, grad_values)


def solution(mesh):
    order = [mesh.axis_names.index("ctx"), mesh.axis_names.index("head")]
    devices = mesh.devices.transpose(order)
    ctx_size, head_size = devices.shape
    chip_mesh = Mesh(devices.reshape(ctx_size // 2, 2, head_size), ("chip", "core", "head"))
    rows = P(("chip", "core"), "head")
    return jax.shard_map(
        body,
        mesh=chip_mesh,
        in_specs=(rows, rows, rows, rows, P(("chip", "core")), P(), P()),
        out_specs=(rows, rows, rows, rows),
        check_vma=False,
    )
```

```python
import functools
import math

import jax
import jax.numpy as jnp
from jax import lax
from jax.experimental import pallas as pl
from jax.experimental.pallas import tpu as pltpu
from jax.sharding import Mesh, PartitionSpec as P

PASSK = 4


def pass_rate(correct, group_size):
    counts = group_size.astype(jnp.float32)
    hit_counts = correct.astype(jnp.float32)
    product = jnp.ones_like(counts)
    for offset in range(PASSK):
        product = product * (counts - hit_counts - offset) / (counts - offset)
    return 1.0 - product


def attention_kernel(
    index_ref, query_ref, grad_ref, mine_ref, other_ref,
    lse_ref, dq_ref, keep_ref, send_ref, *, heads, head_dim, tok_rows, score_scale, tile_blocks,
):
    index = index_ref[0]
    core = index_ref[1]
    pair_rows = tile_blocks * tok_rows
    pair_count = mine_ref.shape[0] * 2 // pair_rows
    last = index // tile_blocks
    rows = heads * tok_rows
    queries = jnp.concatenate(
        [query_ref[:, h * head_dim:(h + 1) * head_dim] for h in range(heads)], 0
    )
    grads = jnp.concatenate(
        [grad_ref[:, h * head_dim:(h + 1) * head_dim] for h in range(heads)], 0
    )
    queries_t = queries.astype(jnp.float32).T.astype(jnp.bfloat16)
    grads_t = grads.astype(jnp.float32).T.astype(jnp.bfloat16)
    key_tok = lax.broadcasted_iota(jnp.int32, (pair_rows, rows), 0)
    row_tok = lax.rem(lax.broadcasted_iota(jnp.int32, (pair_rows, rows), 1), tok_rows)
    visible = key_tok <= row_tok + (index - tile_blocks * last) * tok_rows
    contract_first = (((0,), (0,)), ((), ()))
    lead = core == 0

    def blocks_of(pair):
        parts = []
        for chip in range(tile_blocks // 2):
            source = pl.multiple_of((pair * (tile_blocks // 2) + chip) * tok_rows, tok_rows)
            own = mine_ref[pl.ds(source, tok_rows), :]
            partner = other_ref[pl.ds(source, tok_rows), :]
            parts += [jnp.where(lead, own, partner), jnp.where(lead, partner, own)]
        joined = jnp.concatenate(parts, 0)
        key_block = joined[:, :head_dim]
        value_block = joined[:, head_dim:]
        scores = jnp.dot(key_block, queries_t, preferred_element_type=jnp.float32) * score_scale
        grad_probs = jnp.dot(value_block, grads_t, preferred_element_type=jnp.float32)
        return pl.multiple_of(pair * pair_rows, pair_rows), key_block, scores, grad_probs

    def forward(pair, carry, masked):
        peak, total, weighted = carry
        _, _, scores, grad_probs = blocks_of(pair)
        if masked:
            scores = jnp.where(visible, scores, -1e30)
        new_peak = jnp.maximum(peak, jnp.max(scores, axis=0, keepdims=True))
        exp_terms = jnp.exp(scores - new_peak)
        if masked:
            exp_terms = jnp.where(visible, exp_terms, 0.0)
        shrink = jnp.exp(peak - new_peak)
        total = total * shrink + jnp.sum(exp_terms, axis=0, keepdims=True)
        weighted = weighted * shrink + jnp.sum(exp_terms * grad_probs, axis=0, keepdims=True)
        return new_peak, total, weighted

    start_carry = (
        jnp.full((1, rows), -1e30, jnp.float32),
        jnp.zeros((1, rows), jnp.float32),
        jnp.zeros((1, rows), jnp.float32),
    )
    carry = lax.fori_loop(0, last, lambda b, c: forward(b, c, False), start_carry)
    peak, total, weighted = forward(last, carry, True)
    log_totals = peak + jnp.log(total)
    delta_rows = weighted / total
    lse_ref[...] = log_totals

    def backward(pair, grad_query_t, masked):
        start, key_block, scores, grad_probs = blocks_of(pair)
        probabilities = jnp.exp(scores - log_totals)
        if masked:
            probabilities = jnp.where(visible, probabilities, 0.0)
        grad_scores = (probabilities * (grad_probs - delta_rows)).astype(jnp.bfloat16)
        prob_bf16 = probabilities.astype(jnp.bfloat16)
        grad_query_t = grad_query_t + lax.dot_general(
            key_block, grad_scores, contract_first, preferred_element_type=jnp.float32
        )
        key_add = jnp.dot(grad_scores, queries, preferred_element_type=jnp.float32)
        value_add = jnp.dot(prob_bf16, grads, preferred_element_type=jnp.float32)
        key_add = key_add * score_scale
        for block in range(tile_blocks):
            row = pl.multiple_of((pair * (tile_blocks // 2) + block // 2) * tok_rows, tok_rows)
            part = slice(block * tok_rows, (block + 1) * tok_rows)
            own_first = block % 2 == 0

            @pl.when(lead == own_first)
            def _():
                keep_ref[pl.ds(row, tok_rows), :head_dim] = key_add[part]
                keep_ref[pl.ds(row, tok_rows), head_dim:] = value_add[part]

            @pl.when(lead != own_first)
            def _():
                send_ref[pl.ds(row, tok_rows), :head_dim] = key_add[part]
                send_ref[pl.ds(row, tok_rows), head_dim:] = value_add[part]

        return grad_query_t

    grad_query_t = lax.fori_loop(
        0, last, lambda b, g: backward(b, g, False), jnp.zeros((head_dim, rows), jnp.float32)
    )
    grad_query = (backward(last, grad_query_t, True) * score_scale).T
    for h in range(heads):
        dq_ref[:, h * head_dim:(h + 1) * head_dim] = grad_query[h * tok_rows:(h + 1) * tok_rows]

    def clear(pair, unused):
        half_rows = pair_rows // 2
        start = pl.multiple_of(pair * half_rows, half_rows)
        keep_ref[pl.ds(start, half_rows), :] = jnp.zeros((half_rows, 2 * head_dim), jnp.float32)
        send_ref[pl.ds(start, half_rows), :] = jnp.zeros((half_rows, 2 * head_dim), jnp.float32)
        return unused

    lax.fori_loop(last + 1, pair_count, clear, 0)


def body(queries, key_rows, value_rows, cotangent, trace_ids, correct, group_size):
    tok_rows = queries.shape[0]
    row_width = queries.shape[1]
    head_dim = key_rows.shape[1]
    head_count = row_width // head_dim
    chip_count = lax.axis_size("chip")
    ctx_count = chip_count * 2
    core = lax.axis_index("core")
    my_index = lax.axis_index("chip") * 2 + core
    length = tok_rows * ctx_count
    score_scale = 1.0 / math.sqrt(head_dim)
    pass_rates = pass_rate(correct, group_size)
    traces = jnp.arange(pass_rates.shape[0], dtype=jnp.int32)
    weights = jnp.sum(
        jnp.where(trace_ids[:, None] == traces[None, :], pass_rates[None, :], 0.0), axis=1
    )
    out_grads = (weights[:, None] * cotangent.astype(jnp.float32)).astype(jnp.bfloat16)

    joined = jnp.concatenate([key_rows, value_rows], 1)
    spread = jnp.broadcast_to(joined[None], (chip_count,) + joined.shape)
    mine = lax.all_to_all(spread, "chip", 0, 0, tiled=True)
    other = lax.ppermute(mine, "core", [(0, 1), (1, 0)])
    mine = mine.reshape(chip_count * tok_rows, 2 * head_dim)
    other = other.reshape(chip_count * tok_rows, 2 * head_dim)

    rows = head_count * tok_rows
    vmem = pl.BlockSpec(memory_space=pltpu.MemorySpace.VMEM)
    smem = pl.BlockSpec(memory_space=pltpu.MemorySpace.SMEM)
    kernel = functools.partial(
        attention_kernel, heads=head_count, head_dim=head_dim, tok_rows=tok_rows,
        score_scale=score_scale, tile_blocks=math.gcd(ctx_count, 8),
    )
    stacked_lse, query_grads, keep_part, send_part = pl.pallas_call(
        kernel,
        out_shape=(
            jax.ShapeDtypeStruct((1, rows), jnp.float32),
            jax.ShapeDtypeStruct((tok_rows, row_width), jnp.float32),
            jax.ShapeDtypeStruct((chip_count * tok_rows, 2 * head_dim), jnp.float32),
            jax.ShapeDtypeStruct((chip_count * tok_rows, 2 * head_dim), jnp.float32),
        ),
        in_specs=[smem, vmem, vmem, vmem, vmem],
        out_specs=(vmem, vmem, vmem, vmem),
    )(jnp.stack([my_index, core]).astype(jnp.int32), queries, out_grads, mine, other)
    log_totals = stacked_lse.reshape(head_count, tok_rows).T

    own_part = keep_part + lax.ppermute(send_part, "core", [(0, 1), (1, 0)])
    reduced = jnp.sum(
        lax.all_to_all(own_part.reshape(chip_count, tok_rows, 2 * head_dim), "chip", 0, 0, tiled=True),
        axis=0,
    )
    grad_keys = reduced[:, :head_dim].astype(jnp.bfloat16)
    grad_values = reduced[:, head_dim:].astype(jnp.bfloat16)
    return (log_totals, query_grads, grad_keys, grad_values)


def solution(mesh):
    order = [mesh.axis_names.index("ctx"), mesh.axis_names.index("head")]
    devices = mesh.devices.transpose(order)
    ctx_size, head_size = devices.shape
    chip_mesh = Mesh(devices.reshape(ctx_size // 2, 2, head_size), ("chip", "core", "head"))
    rows = P(("chip", "core"), "head")
    return jax.shard_map(
        body,
        mesh=chip_mesh,
        in_specs=(rows, rows, rows, rows, P(("chip", "core")), P(), P()),
        out_specs=(rows, rows, rows, rows),
        check_vma=False,
    )
```

```python
import functools
import math

import jax
import jax.numpy as jnp
from jax import lax
from jax.experimental import pallas as pl
from jax.experimental.pallas import tpu as pltpu
from jax.sharding import Mesh, PartitionSpec as P

PASSK = 4


def pass_rate(correct, group_size):
    counts = group_size.astype(jnp.float32)
    hit_counts = correct.astype(jnp.float32)
    product = jnp.ones_like(counts)
    for offset in range(PASSK):
        product = product * (counts - hit_counts - offset) / (counts - offset)
    return 1.0 - product


def attention_kernel(
    index_ref, query_ref, weight_ref, cotangent_ref, mine_ref, other_ref,
    lse_ref, dq_ref, keep_ref, send_ref, *, heads, head_dim, tok_rows, score_scale, tile_blocks,
):
    index = index_ref[0]
    core = index_ref[1]
    pair_rows = tile_blocks * tok_rows
    pair_count = mine_ref.shape[0] * 2 // pair_rows
    last = index // tile_blocks
    rows = heads * tok_rows
    queries = jnp.concatenate(
        [query_ref[:, h * head_dim:(h + 1) * head_dim] for h in range(heads)], 0
    )
    weights = weight_ref[...]
    grads = jnp.concatenate(
        [
            (weights * cotangent_ref[:, h * head_dim:(h + 1) * head_dim].astype(jnp.float32)).astype(jnp.bfloat16)
            for h in range(heads)
        ],
        0,
    )
    queries_t = queries.astype(jnp.float32).T.astype(jnp.bfloat16)
    grads_t = grads.astype(jnp.float32).T.astype(jnp.bfloat16)
    key_tok = lax.broadcasted_iota(jnp.int32, (pair_rows, rows), 0)
    row_tok = lax.rem(lax.broadcasted_iota(jnp.int32, (pair_rows, rows), 1), tok_rows)
    visible = key_tok <= row_tok + (index - tile_blocks * last) * tok_rows
    contract_first = (((0,), (0,)), ((), ()))
    lead = core == 0

    def blocks_of(pair):
        parts = []
        for chip in range(tile_blocks // 2):
            source = pl.multiple_of((pair * (tile_blocks // 2) + chip) * tok_rows, tok_rows)
            own = mine_ref[pl.ds(source, tok_rows), :]
            partner = other_ref[pl.ds(source, tok_rows), :]
            parts += [jnp.where(lead, own, partner), jnp.where(lead, partner, own)]
        joined = jnp.concatenate(parts, 0)
        key_block = joined[:, :head_dim]
        value_block = joined[:, head_dim:]
        scores = jnp.dot(key_block, queries_t, preferred_element_type=jnp.float32) * score_scale
        grad_probs = jnp.dot(value_block, grads_t, preferred_element_type=jnp.float32)
        return pl.multiple_of(pair * pair_rows, pair_rows), key_block, scores, grad_probs

    def forward(pair, carry, masked):
        peak, total, weighted = carry
        _, _, scores, grad_probs = blocks_of(pair)
        if masked:
            scores = jnp.where(visible, scores, -1e30)
        new_peak = jnp.maximum(peak, jnp.max(scores, axis=0, keepdims=True))
        exp_terms = jnp.exp(scores - new_peak)
        if masked:
            exp_terms = jnp.where(visible, exp_terms, 0.0)
        shrink = jnp.exp(peak - new_peak)
        total = total * shrink + jnp.sum(exp_terms, axis=0, keepdims=True)
        weighted = weighted * shrink + jnp.sum(exp_terms * grad_probs, axis=0, keepdims=True)
        return new_peak, total, weighted

    start_carry = (
        jnp.full((1, rows), -1e30, jnp.float32),
        jnp.zeros((1, rows), jnp.float32),
        jnp.zeros((1, rows), jnp.float32),
    )
    carry = lax.fori_loop(0, last, lambda b, c: forward(b, c, False), start_carry)
    peak, total, weighted = forward(last, carry, True)
    log_totals = peak + jnp.log(total)
    delta_rows = weighted / total
    lse_ref[...] = log_totals

    def backward(pair, grad_query_t, masked):
        start, key_block, scores, grad_probs = blocks_of(pair)
        probabilities = jnp.exp(scores - log_totals)
        if masked:
            probabilities = jnp.where(visible, probabilities, 0.0)
        grad_scores = (probabilities * (grad_probs - delta_rows)).astype(jnp.bfloat16)
        prob_bf16 = probabilities.astype(jnp.bfloat16)
        grad_query_t = grad_query_t + lax.dot_general(
            key_block, grad_scores, contract_first, preferred_element_type=jnp.float32
        )
        key_add = jnp.dot(grad_scores, queries, preferred_element_type=jnp.float32)
        value_add = jnp.dot(prob_bf16, grads, preferred_element_type=jnp.float32)
        key_add = key_add * score_scale
        for block in range(tile_blocks):
            row = pl.multiple_of((pair * (tile_blocks // 2) + block // 2) * tok_rows, tok_rows)
            part = slice(block * tok_rows, (block + 1) * tok_rows)
            own_first = block % 2 == 0

            @pl.when(lead == own_first)
            def _():
                keep_ref[pl.ds(row, tok_rows), :head_dim] = key_add[part]
                keep_ref[pl.ds(row, tok_rows), head_dim:] = value_add[part]

            @pl.when(lead != own_first)
            def _():
                send_ref[pl.ds(row, tok_rows), :head_dim] = key_add[part]
                send_ref[pl.ds(row, tok_rows), head_dim:] = value_add[part]

        return grad_query_t

    grad_query_t = lax.fori_loop(
        0, last, lambda b, g: backward(b, g, False), jnp.zeros((head_dim, rows), jnp.float32)
    )
    grad_query = (backward(last, grad_query_t, True) * score_scale).T
    for h in range(heads):
        dq_ref[:, h * head_dim:(h + 1) * head_dim] = grad_query[h * tok_rows:(h + 1) * tok_rows]

    def clear(pair, unused):
        half_rows = pair_rows // 2
        start = pl.multiple_of(pair * half_rows, half_rows)
        keep_ref[pl.ds(start, half_rows), :] = jnp.zeros((half_rows, 2 * head_dim), jnp.float32)
        send_ref[pl.ds(start, half_rows), :] = jnp.zeros((half_rows, 2 * head_dim), jnp.float32)
        return unused

    lax.fori_loop(last + 1, pair_count, clear, 0)


def add_kernel(first_ref, second_ref, out_ref):
    out_ref[...] = first_ref[...] + second_ref[...]


def body(queries, key_rows, value_rows, cotangent, trace_ids, correct, group_size):
    tok_rows = queries.shape[0]
    row_width = queries.shape[1]
    head_dim = key_rows.shape[1]
    head_count = row_width // head_dim
    chip_count = lax.axis_size("chip")
    ctx_count = chip_count * 2
    core = lax.axis_index("core")
    my_index = lax.axis_index("chip") * 2 + core
    length = tok_rows * ctx_count
    score_scale = 1.0 / math.sqrt(head_dim)
    pass_rates = pass_rate(correct, group_size)
    traces = jnp.arange(pass_rates.shape[0], dtype=jnp.int32)
    weights = jnp.sum(
        jnp.where(trace_ids[:, None] == traces[None, :], pass_rates[None, :], 0.0), axis=1
    )

    joined = jnp.concatenate([key_rows, value_rows], 1)
    spread = jnp.broadcast_to(joined[None], (chip_count,) + joined.shape)
    mine = lax.all_to_all(spread, "chip", 0, 0, tiled=True)
    other = lax.ppermute(mine, "core", [(0, 1), (1, 0)])
    mine = mine.reshape(chip_count * tok_rows, 2 * head_dim)
    other = other.reshape(chip_count * tok_rows, 2 * head_dim)

    rows = head_count * tok_rows
    vmem = pl.BlockSpec(memory_space=pltpu.MemorySpace.VMEM)
    smem = pl.BlockSpec(memory_space=pltpu.MemorySpace.SMEM)
    kernel = functools.partial(
        attention_kernel, heads=head_count, head_dim=head_dim, tok_rows=tok_rows,
        score_scale=score_scale, tile_blocks=math.gcd(ctx_count, 8),
    )
    stacked_lse, query_grads, keep_part, send_part = pl.pallas_call(
        kernel,
        out_shape=(
            jax.ShapeDtypeStruct((1, rows), jnp.float32),
            jax.ShapeDtypeStruct((tok_rows, row_width), jnp.float32),
            jax.ShapeDtypeStruct((chip_count * tok_rows, 2 * head_dim), jnp.float32),
            jax.ShapeDtypeStruct((chip_count * tok_rows, 2 * head_dim), jnp.float32),
        ),
        in_specs=[smem, vmem, vmem, vmem, vmem, vmem],
        out_specs=(vmem, vmem, vmem, vmem),
    )(jnp.stack([my_index, core]).astype(jnp.int32), queries, weights[:, None], cotangent, mine, other)
    log_totals = stacked_lse.reshape(head_count, tok_rows).T

    swapped = lax.ppermute(send_part, "core", [(0, 1), (1, 0)])
    own_part = pl.pallas_call(
        add_kernel,
        out_shape=jax.ShapeDtypeStruct(keep_part.shape, jnp.float32),
        in_specs=[vmem, vmem],
        out_specs=vmem,
    )(keep_part, swapped)
    reduced = jnp.sum(
        lax.all_to_all(own_part.reshape(chip_count, tok_rows, 2 * head_dim), "chip", 0, 0, tiled=True),
        axis=0,
    )
    grad_keys = reduced[:, :head_dim].astype(jnp.bfloat16)
    grad_values = reduced[:, head_dim:].astype(jnp.bfloat16)
    return (log_totals, query_grads, grad_keys, grad_values)


def solution(mesh):
    order = [mesh.axis_names.index("ctx"), mesh.axis_names.index("head")]
    devices = mesh.devices.transpose(order)
    ctx_size, head_size = devices.shape
    chip_mesh = Mesh(devices.reshape(ctx_size // 2, 2, head_size), ("chip", "core", "head"))
    rows = P(("chip", "core"), "head")
    return jax.shard_map(
        body,
        mesh=chip_mesh,
        in_specs=(rows, rows, rows, rows, P(("chip", "core")), P(), P()),
        out_specs=(rows, rows, rows, rows),
        check_vma=False,
    )
```

```python
import functools
import math

import jax
import jax.numpy as jnp
from jax import lax
from jax.experimental import pallas as pl
from jax.experimental.pallas import tpu as pltpu
from jax.sharding import Mesh, PartitionSpec as P

PASSK = 4
LOG2_E = 1.4426950408889634
LN_2 = 0.6931471805599453


def pass_rate(correct, group_size):
    counts = group_size.astype(jnp.float32)
    hit_counts = correct.astype(jnp.float32)
    product = jnp.ones_like(counts)
    for offset in range(PASSK):
        product = product * (counts - hit_counts - offset) / (counts - offset)
    return 1.0 - product


def attention_kernel(
    index_ref, query_ref, grad_ref, mine_ref, other_ref,
    lse_ref, dq_ref, dk_ref, dv_ref, *, heads, head_dim, tok_rows, score_scale, tile_blocks,
):
    index = index_ref[0]
    core = index_ref[1]
    pair_rows = tile_blocks * tok_rows
    pair_count = mine_ref.shape[0] * 2 // pair_rows
    last = index // tile_blocks
    rows = heads * tok_rows
    queries = jnp.concatenate(
        [query_ref[:, h * head_dim:(h + 1) * head_dim] for h in range(heads)], 0
    )
    grads = jnp.concatenate(
        [grad_ref[:, h * head_dim:(h + 1) * head_dim] for h in range(heads)], 0
    )
    queries_t = queries.astype(jnp.float32).T.astype(jnp.bfloat16)
    grads_t = grads.astype(jnp.float32).T.astype(jnp.bfloat16)
    key_tok = lax.broadcasted_iota(jnp.int32, (pair_rows, rows), 0)
    row_tok = lax.rem(lax.broadcasted_iota(jnp.int32, (pair_rows, rows), 1), tok_rows)
    visible = key_tok <= row_tok + (index - tile_blocks * last) * tok_rows
    contract_first = (((0,), (0,)), ((), ()))
    lead = core == 0

    def blocks_of(pair):
        parts = []
        for chip in range(tile_blocks // 2):
            source = pl.multiple_of((pair * (tile_blocks // 2) + chip) * tok_rows, tok_rows)
            own = mine_ref[pl.ds(source, tok_rows), :]
            partner = other_ref[pl.ds(source, tok_rows), :]
            parts += [jnp.where(lead, own, partner), jnp.where(lead, partner, own)]
        joined = jnp.concatenate(parts, 0)
        key_block = joined[:, :head_dim]
        value_block = joined[:, head_dim:]
        scores = jnp.dot(key_block, queries_t, preferred_element_type=jnp.float32) * (score_scale * LOG2_E)
        grad_probs = jnp.dot(value_block, grads_t, preferred_element_type=jnp.float32)
        return pl.multiple_of(pair * pair_rows, pair_rows), key_block, scores, grad_probs

    def forward(pair, carry, masked):
        peak, total, weighted = carry
        _, _, scores, grad_probs = blocks_of(pair)
        if masked:
            scores = jnp.where(visible, scores, -1e30)
        new_peak = jnp.maximum(peak, jnp.max(scores, axis=0, keepdims=True))
        exp_terms = jnp.exp2(scores - new_peak)
        if masked:
            exp_terms = jnp.where(visible, exp_terms, 0.0)
        shrink = jnp.exp2(peak - new_peak)
        total = total * shrink + jnp.sum(exp_terms, axis=0, keepdims=True)
        weighted = weighted * shrink + jnp.sum(exp_terms * grad_probs, axis=0, keepdims=True)
        return new_peak, total, weighted

    start_carry = (
        jnp.full((1, rows), -1e30, jnp.float32),
        jnp.zeros((1, rows), jnp.float32),
        jnp.zeros((1, rows), jnp.float32),
    )
    carry = lax.fori_loop(0, last, lambda b, c: forward(b, c, False), start_carry)
    peak, total, weighted = forward(last, carry, True)
    log_totals = peak + jnp.log2(total)
    delta_rows = weighted / total
    lse_ref[...] = log_totals * LN_2

    def backward(pair, grad_query_t, masked):
        start, key_block, scores, grad_probs = blocks_of(pair)
        probabilities = jnp.exp2(scores - log_totals)
        if masked:
            probabilities = jnp.where(visible, probabilities, 0.0)
        grad_scores = (probabilities * (grad_probs - delta_rows)).astype(jnp.bfloat16)
        prob_bf16 = probabilities.astype(jnp.bfloat16)
        grad_query_t = grad_query_t + lax.dot_general(
            key_block, grad_scores, contract_first, preferred_element_type=jnp.float32
        )
        key_add = jnp.dot(grad_scores, queries, preferred_element_type=jnp.float32)
        value_add = jnp.dot(prob_bf16, grads, preferred_element_type=jnp.float32)
        dk_ref[pl.ds(start, pair_rows), :] = key_add * score_scale
        dv_ref[pl.ds(start, pair_rows), :] = value_add
        return grad_query_t

    grad_query_t = lax.fori_loop(
        0, last, lambda b, g: backward(b, g, False), jnp.zeros((head_dim, rows), jnp.float32)
    )
    grad_query = (backward(last, grad_query_t, True) * score_scale).T
    for h in range(heads):
        dq_ref[:, h * head_dim:(h + 1) * head_dim] = grad_query[h * tok_rows:(h + 1) * tok_rows]

    def clear(pair, unused):
        start = pl.multiple_of(pair * pair_rows, pair_rows)
        dk_ref[pl.ds(start, pair_rows), :] = jnp.zeros((pair_rows, head_dim), jnp.float32)
        dv_ref[pl.ds(start, pair_rows), :] = jnp.zeros((pair_rows, head_dim), jnp.float32)
        return unused

    lax.fori_loop(last + 1, pair_count, clear, 0)


def body(queries, key_rows, value_rows, cotangent, trace_ids, correct, group_size):
    tok_rows = queries.shape[0]
    row_width = queries.shape[1]
    head_dim = key_rows.shape[1]
    head_count = row_width // head_dim
    chip_count = lax.axis_size("chip")
    ctx_count = chip_count * 2
    core = lax.axis_index("core")
    my_index = lax.axis_index("chip") * 2 + core
    length = tok_rows * ctx_count
    score_scale = 1.0 / math.sqrt(head_dim)
    pass_rates = pass_rate(correct, group_size)
    traces = jnp.arange(pass_rates.shape[0], dtype=jnp.int32)
    weights = jnp.sum(
        jnp.where(trace_ids[:, None] == traces[None, :], pass_rates[None, :], 0.0), axis=1
    )
    out_grads = (weights[:, None] * cotangent.astype(jnp.float32)).astype(jnp.bfloat16)

    joined = jnp.concatenate([key_rows, value_rows], 1)
    spread = jnp.broadcast_to(joined[None], (chip_count,) + joined.shape)
    mine = lax.all_to_all(spread, "chip", 0, 0, tiled=True)
    other = lax.ppermute(mine, "core", [(0, 1), (1, 0)])
    mine = mine.reshape(chip_count * tok_rows, 2 * head_dim)
    other = other.reshape(chip_count * tok_rows, 2 * head_dim)

    rows = head_count * tok_rows
    vmem = pl.BlockSpec(memory_space=pltpu.MemorySpace.VMEM)
    smem = pl.BlockSpec(memory_space=pltpu.MemorySpace.SMEM)
    kernel = functools.partial(
        attention_kernel, heads=head_count, head_dim=head_dim, tok_rows=tok_rows,
        score_scale=score_scale, tile_blocks=math.gcd(ctx_count, 8),
    )
    stacked_lse, query_grads, key_part, value_part = pl.pallas_call(
        kernel,
        out_shape=(
            jax.ShapeDtypeStruct((1, rows), jnp.float32),
            jax.ShapeDtypeStruct((tok_rows, row_width), jnp.float32),
            jax.ShapeDtypeStruct((length, head_dim), jnp.float32),
            jax.ShapeDtypeStruct((length, head_dim), jnp.float32),
        ),
        in_specs=[smem, vmem, vmem, vmem, vmem],
        out_specs=(vmem, vmem, vmem, vmem),
    )(jnp.stack([my_index, core]).astype(jnp.int32), queries, out_grads, mine, other)
    log_totals = stacked_lse.reshape(head_count, tok_rows).T

    chip_rows = 2 * tok_rows
    key_part = key_part.reshape(chip_count, chip_rows, head_dim)
    value_part = value_part.reshape(chip_count, chip_rows, head_dim)
    lead = core == 0
    swapped = lax.ppermute(jnp.where(lead, value_part, key_part), "core", [(0, 1), (1, 0)])
    own_part = jnp.where(lead, key_part, value_part) + swapped
    reduced = jnp.sum(lax.all_to_all(own_part, "chip", 0, 0, tiled=True), axis=0).astype(jnp.bfloat16)
    other = lax.ppermute(
        jnp.where(lead, reduced[tok_rows:], reduced[:tok_rows]), "core", [(0, 1), (1, 0)]
    )
    grad_keys = jnp.where(lead, reduced[:tok_rows], other)
    grad_values = jnp.where(lead, other, reduced[tok_rows:])
    return (log_totals, query_grads, grad_keys, grad_values)


def solution(mesh):
    order = [mesh.axis_names.index("ctx"), mesh.axis_names.index("head")]
    devices = mesh.devices.transpose(order)
    ctx_size, head_size = devices.shape
    chip_mesh = Mesh(devices.reshape(ctx_size // 2, 2, head_size), ("chip", "core", "head"))
    rows = P(("chip", "core"), "head")
    return jax.shard_map(
        body,
        mesh=chip_mesh,
        in_specs=(rows, rows, rows, rows, P(("chip", "core")), P(), P()),
        out_specs=(rows, rows, rows, rows),
        check_vma=False,
    )
```

```python
import functools
import math

import jax
import jax.numpy as jnp
from jax import lax
from jax.experimental import pallas as pl
from jax.experimental.pallas import tpu as pltpu
from jax.sharding import Mesh, PartitionSpec as P

PASSK = 4
LOG2_E = 1.4426950408889634
LN_2 = 0.6931471805599453


def pass_rate(correct, group_size):
    counts = group_size.astype(jnp.float32)
    hit_counts = correct.astype(jnp.float32)
    product = jnp.ones_like(counts)
    for offset in range(PASSK):
        product = product * (counts - hit_counts - offset) / (counts - offset)
    return 1.0 - product


def attention_kernel(
    index_ref, query_ref, grad_ref, mine_ref, other_ref,
    lse_ref, dq_ref, dk_ref, dv_ref, *, heads, head_dim, tok_rows, score_scale, tile_blocks,
):
    index = index_ref[0]
    core = index_ref[1]
    pair_rows = tile_blocks * tok_rows
    pair_count = mine_ref.shape[0] * 2 // pair_rows
    last = index // tile_blocks
    rows = heads * tok_rows
    queries = jnp.concatenate(
        [query_ref[:, h * head_dim:(h + 1) * head_dim] for h in range(heads)], 0
    )
    grads = jnp.concatenate(
        [grad_ref[:, h * head_dim:(h + 1) * head_dim] for h in range(heads)], 0
    )
    queries_t = queries.astype(jnp.float32).T.astype(jnp.bfloat16)
    grads_t = grads.astype(jnp.float32).T.astype(jnp.bfloat16)
    shift = (index - tile_blocks * last) * tok_rows

    def visible():
        key_tok = lax.broadcasted_iota(jnp.int32, (pair_rows, rows), 0)
        lane = lax.broadcasted_iota(jnp.int32, (pair_rows, rows), 1)
        if tok_rows & (tok_rows - 1) == 0:
            row_tok = jnp.bitwise_and(lane, tok_rows - 1)
        else:
            row_tok = lax.rem(lane, tok_rows)
        return key_tok <= row_tok + shift
    contract_first = (((0,), (0,)), ((), ()))
    lead = core == 0

    def blocks_of(pair):
        parts = []
        for chip in range(tile_blocks // 2):
            source = pl.multiple_of((pair * (tile_blocks // 2) + chip) * tok_rows, tok_rows)
            own = mine_ref[pl.ds(source, tok_rows), :]
            partner = other_ref[pl.ds(source, tok_rows), :]
            parts += [jnp.where(lead, own, partner), jnp.where(lead, partner, own)]
        joined = jnp.concatenate(parts, 0)
        key_block = joined[:, :head_dim]
        value_block = joined[:, head_dim:]
        scores = jnp.dot(key_block, queries_t, preferred_element_type=jnp.float32) * (score_scale * LOG2_E)
        grad_probs = jnp.dot(value_block, grads_t, preferred_element_type=jnp.float32)
        return pl.multiple_of(pair * pair_rows, pair_rows), key_block, scores, grad_probs

    def forward(pair, carry, masked):
        peak, total, weighted = carry
        _, _, scores, grad_probs = blocks_of(pair)
        if masked:
            mask = visible()
            scores = jnp.where(mask, scores, -1e30)
        new_peak = jnp.maximum(peak, jnp.max(scores, axis=0, keepdims=True))
        exp_terms = jnp.exp2(scores - new_peak)
        if masked:
            exp_terms = jnp.where(mask, exp_terms, 0.0)
        shrink = jnp.exp2(peak - new_peak)
        total = total * shrink + jnp.sum(exp_terms, axis=0, keepdims=True)
        weighted = weighted * shrink + jnp.sum(exp_terms * grad_probs, axis=0, keepdims=True)
        return new_peak, total, weighted

    start_carry = (
        jnp.full((1, rows), -1e30, jnp.float32),
        jnp.zeros((1, rows), jnp.float32),
        jnp.zeros((1, rows), jnp.float32),
    )
    carry = lax.fori_loop(0, last, lambda b, c: forward(b, c, False), start_carry)
    peak, total, weighted = forward(last, carry, True)
    log_totals = peak + jnp.log2(total)
    delta_rows = weighted / total
    lse_ref[...] = log_totals * LN_2

    def backward(pair, grad_query_t, masked):
        start, key_block, scores, grad_probs = blocks_of(pair)
        probabilities = jnp.exp2(scores - log_totals)
        if masked:
            probabilities = jnp.where(visible(), probabilities, 0.0)
        grad_scores = (probabilities * (grad_probs - delta_rows)).astype(jnp.bfloat16)
        prob_bf16 = probabilities.astype(jnp.bfloat16)
        grad_query_t = grad_query_t + lax.dot_general(
            key_block, grad_scores, contract_first, preferred_element_type=jnp.float32
        )
        key_add = jnp.dot(grad_scores, queries, preferred_element_type=jnp.float32)
        value_add = jnp.dot(prob_bf16, grads, preferred_element_type=jnp.float32)
        dk_ref[pl.ds(start, pair_rows), :] = key_add * score_scale
        dv_ref[pl.ds(start, pair_rows), :] = value_add
        return grad_query_t

    grad_query_t = lax.fori_loop(
        0, last, lambda b, g: backward(b, g, False), jnp.zeros((head_dim, rows), jnp.float32)
    )
    grad_query = (backward(last, grad_query_t, True) * score_scale).T
    for h in range(heads):
        dq_ref[:, h * head_dim:(h + 1) * head_dim] = grad_query[h * tok_rows:(h + 1) * tok_rows]

    def clear(pair, unused):
        start = pl.multiple_of(pair * pair_rows, pair_rows)
        dk_ref[pl.ds(start, pair_rows), :] = jnp.zeros((pair_rows, head_dim), jnp.float32)
        dv_ref[pl.ds(start, pair_rows), :] = jnp.zeros((pair_rows, head_dim), jnp.float32)
        return unused

    lax.fori_loop(last + 1, pair_count, clear, 0)


def body(queries, key_rows, value_rows, cotangent, trace_ids, correct, group_size):
    tok_rows = queries.shape[0]
    row_width = queries.shape[1]
    head_dim = key_rows.shape[1]
    head_count = row_width // head_dim
    chip_count = lax.axis_size("chip")
    ctx_count = chip_count * 2
    core = lax.axis_index("core")
    my_index = lax.axis_index("chip") * 2 + core
    length = tok_rows * ctx_count
    score_scale = 1.0 / math.sqrt(head_dim)
    pass_rates = pass_rate(correct, group_size)
    traces = jnp.arange(pass_rates.shape[0], dtype=jnp.int32)
    weights = jnp.sum(
        jnp.where(trace_ids[:, None] == traces[None, :], pass_rates[None, :], 0.0), axis=1
    )
    out_grads = (weights[:, None] * cotangent.astype(jnp.float32)).astype(jnp.bfloat16)

    joined = jnp.concatenate([key_rows, value_rows], 1)
    spread = jnp.broadcast_to(joined[None], (chip_count,) + joined.shape)
    mine = lax.all_to_all(spread, "chip", 0, 0, tiled=True)
    other = lax.ppermute(mine, "core", [(0, 1), (1, 0)])
    mine = mine.reshape(chip_count * tok_rows, 2 * head_dim)
    other = other.reshape(chip_count * tok_rows, 2 * head_dim)

    rows = head_count * tok_rows
    vmem = pl.BlockSpec(memory_space=pltpu.MemorySpace.VMEM)
    smem = pl.BlockSpec(memory_space=pltpu.MemorySpace.SMEM)
    kernel = functools.partial(
        attention_kernel, heads=head_count, head_dim=head_dim, tok_rows=tok_rows,
        score_scale=score_scale, tile_blocks=math.gcd(ctx_count, 8),
    )
    stacked_lse, query_grads, key_part, value_part = pl.pallas_call(
        kernel,
        out_shape=(
            jax.ShapeDtypeStruct((1, rows), jnp.float32),
            jax.ShapeDtypeStruct((tok_rows, row_width), jnp.float32),
            jax.ShapeDtypeStruct((length, head_dim), jnp.float32),
            jax.ShapeDtypeStruct((length, head_dim), jnp.float32),
        ),
        in_specs=[smem, vmem, vmem, vmem, vmem],
        out_specs=(vmem, vmem, vmem, vmem),
    )(jnp.stack([my_index, core]).astype(jnp.int32), queries, out_grads, mine, other)
    log_totals = stacked_lse.reshape(head_count, tok_rows).T

    chip_rows = 2 * tok_rows
    key_part = key_part.reshape(chip_count, chip_rows, head_dim)
    value_part = value_part.reshape(chip_count, chip_rows, head_dim)
    lead = core == 0
    swapped = lax.ppermute(jnp.where(lead, value_part, key_part), "core", [(0, 1), (1, 0)])
    own_part = jnp.where(lead, key_part, value_part) + swapped
    reduced = jnp.sum(lax.all_to_all(own_part, "chip", 0, 0, tiled=True), axis=0).astype(jnp.bfloat16)
    other = lax.ppermute(
        jnp.where(lead, reduced[tok_rows:], reduced[:tok_rows]), "core", [(0, 1), (1, 0)]
    )
    grad_keys = jnp.where(lead, reduced[:tok_rows], other)
    grad_values = jnp.where(lead, other, reduced[tok_rows:])
    return (log_totals, query_grads, grad_keys, grad_values)


def solution(mesh):
    order = [mesh.axis_names.index("ctx"), mesh.axis_names.index("head")]
    devices = mesh.devices.transpose(order)
    ctx_size, head_size = devices.shape
    chip_mesh = Mesh(devices.reshape(ctx_size // 2, 2, head_size), ("chip", "core", "head"))
    rows = P(("chip", "core"), "head")
    return jax.shard_map(
        body,
        mesh=chip_mesh,
        in_specs=(rows, rows, rows, rows, P(("chip", "core")), P(), P()),
        out_specs=(rows, rows, rows, rows),
        check_vma=False,
    )
```

```python
import functools
import math

import jax
import jax.numpy as jnp
from jax import lax
from jax.experimental import pallas as pl
from jax.experimental.pallas import tpu as pltpu
from jax.sharding import Mesh, PartitionSpec as P

PASSK = 4
LOG2_E = 1.4426950408889634
LN_2 = 0.6931471805599453


def pass_rate(correct, group_size):
    counts = group_size.astype(jnp.float32)
    hit_counts = correct.astype(jnp.float32)
    product = jnp.ones_like(counts)
    for offset in range(PASSK):
        product = product * (counts - hit_counts - offset) / (counts - offset)
    return 1.0 - product


def stacked_rows(index_ref, own_ref, partner_ref, heads, head_dim, column):
    lead = index_ref[1] == 0
    first = jnp.where(lead, own_ref[...], partner_ref[...])
    second = jnp.where(lead, partner_ref[...], own_ref[...])
    base = column * heads * head_dim
    return jnp.concatenate(
        [
            block[:, base + h * head_dim:base + (h + 1) * head_dim]
            for block in (first, second)
            for h in range(heads)
        ],
        0,
    )


def tile_parts(index_ref, mine_ref, tile, tile_chips, tok_rows, heads, head_dim, score_scale, queries_t, grads_t):
    source = pl.multiple_of(tile * tile_chips * tok_rows, tok_rows)
    joined = mine_ref[pl.ds(source, tile_chips * tok_rows), :]
    key_block = joined[:, :head_dim]
    value_block = joined[:, head_dim:]
    scores = jnp.dot(key_block, queries_t, preferred_element_type=jnp.float32) * (score_scale * LOG2_E)
    grad_probs = jnp.dot(value_block, grads_t, preferred_element_type=jnp.float32)
    return key_block, scores, grad_probs


def visible_of(index_ref, tile, tile_chips, tok_rows, heads):
    chip = index_ref[0]
    core = index_ref[1]
    rows = 2 * heads * tok_rows
    key_row = lax.broadcasted_iota(jnp.int32, (tile_chips * tok_rows, 1), 0)
    lane = lax.broadcasted_iota(jnp.int32, (1, rows), 1)
    key_chip = tile * tile_chips + key_row // tok_rows
    key_pos = (2 * key_chip + core) * tok_rows + key_row % tok_rows
    query_block = (lane >= heads * tok_rows).astype(jnp.int32)
    query_pos = (2 * chip + query_block) * tok_rows + lane % tok_rows
    return key_pos <= query_pos


def forward_kernel(index_ref, own_ref, partner_ref, mine_ref, stats_ref, *, heads, head_dim, tok_rows, score_scale, tile_chips):
    chip = index_ref[0]
    last = chip // tile_chips
    rows = 2 * heads * tok_rows
    queries_t = stacked_rows(index_ref, own_ref, partner_ref, heads, head_dim, 0).astype(jnp.float32).T.astype(jnp.bfloat16)
    grads_t = stacked_rows(index_ref, own_ref, partner_ref, heads, head_dim, 1).astype(jnp.float32).T.astype(jnp.bfloat16)

    def forward(tile, carry, masked):
        peak, total, weighted = carry
        _, scores, grad_probs = tile_parts(
            index_ref, mine_ref, tile, tile_chips, tok_rows, heads, head_dim, score_scale, queries_t, grads_t
        )
        if masked:
            mask = visible_of(index_ref, tile, tile_chips, tok_rows, heads)
            scores = jnp.where(mask, scores, -1e30)
        new_peak = jnp.maximum(peak, jnp.max(scores, axis=0, keepdims=True))
        exp_terms = jnp.exp2(scores - new_peak)
        if masked:
            exp_terms = jnp.where(mask, exp_terms, 0.0)
        shrink = jnp.exp2(peak - new_peak)
        total = total * shrink + jnp.sum(exp_terms, axis=0, keepdims=True)
        weighted = weighted * shrink + jnp.sum(exp_terms * grad_probs, axis=0, keepdims=True)
        return new_peak, total, weighted

    start_carry = (
        jnp.full((1, rows), -1e30, jnp.float32),
        jnp.zeros((1, rows), jnp.float32),
        jnp.zeros((1, rows), jnp.float32),
    )
    carry = lax.fori_loop(0, last, lambda b, c: forward(b, c, False), start_carry)
    peak, total, weighted = forward(last, carry, True)
    stats_ref[0:1, :] = peak
    stats_ref[1:2, :] = total
    stats_ref[2:3, :] = weighted


def backward_kernel(
    index_ref, own_ref, partner_ref, mine_ref, stats_ref, partner_stats_ref, lse_ref, dq_ref, part_ref,
    *, heads, head_dim, tok_rows, score_scale, tile_chips,
):
    chip = index_ref[0]
    last = chip // tile_chips
    tile_count = mine_ref.shape[0] // (tile_chips * tok_rows)
    rows = 2 * heads * tok_rows
    queries = stacked_rows(index_ref, own_ref, partner_ref, heads, head_dim, 0)
    grads = stacked_rows(index_ref, own_ref, partner_ref, heads, head_dim, 1)
    queries_t = queries.astype(jnp.float32).T.astype(jnp.bfloat16)
    grads_t = grads.astype(jnp.float32).T.astype(jnp.bfloat16)
    peak = jnp.maximum(stats_ref[0:1, :], partner_stats_ref[0:1, :])
    own_shrink = jnp.exp2(stats_ref[0:1, :] - peak)
    partner_shrink = jnp.exp2(partner_stats_ref[0:1, :] - peak)
    total = stats_ref[1:2, :] * own_shrink + partner_stats_ref[1:2, :] * partner_shrink
    weighted = stats_ref[2:3, :] * own_shrink + partner_stats_ref[2:3, :] * partner_shrink
    log_totals = peak + jnp.log2(total)
    delta_rows = weighted / total
    lse_ref[...] = log_totals
    contract_first = (((0,), (0,)), ((), ()))
    tile_rows = tile_chips * tok_rows

    def backward(tile, grad_query_t, masked):
        key_block, scores, grad_probs = tile_parts(
            index_ref, mine_ref, tile, tile_chips, tok_rows, heads, head_dim, score_scale, queries_t, grads_t
        )
        probabilities = jnp.exp2(scores - log_totals)
        if masked:
            probabilities = jnp.where(visible_of(index_ref, tile, tile_chips, tok_rows, heads), probabilities, 0.0)
        grad_scores = (probabilities * (grad_probs - delta_rows)).astype(jnp.bfloat16)
        prob_bf16 = probabilities.astype(jnp.bfloat16)
        grad_query_t = grad_query_t + lax.dot_general(
            key_block, grad_scores, contract_first, preferred_element_type=jnp.float32
        )
        key_add = jnp.dot(grad_scores, queries, preferred_element_type=jnp.float32)
        value_add = jnp.dot(prob_bf16, grads, preferred_element_type=jnp.float32)
        start = pl.multiple_of(tile * tile_rows, tile_rows)
        part_ref[pl.ds(start, tile_rows), :head_dim] = key_add * score_scale
        part_ref[pl.ds(start, tile_rows), head_dim:] = value_add
        return grad_query_t

    grad_query_t = lax.fori_loop(
        0, last, lambda b, g: backward(b, g, False), jnp.zeros((head_dim, rows), jnp.float32)
    )
    grad_query = (backward(last, grad_query_t, True) * score_scale).T
    for block in range(2):
        for h in range(heads):
            row = (block * heads + h) * tok_rows
            dq_ref[block * tok_rows:(block + 1) * tok_rows, h * head_dim:(h + 1) * head_dim] = (
                grad_query[row:row + tok_rows]
            )

    def clear(tile, unused):
        start = pl.multiple_of(tile * tile_rows, tile_rows)
        part_ref[pl.ds(start, tile_rows), :] = jnp.zeros((tile_rows, 2 * head_dim), jnp.float32)
        return unused

    lax.fori_loop(last + 1, tile_count, clear, 0)


def body(queries, key_rows, value_rows, cotangent, trace_ids, correct, group_size):
    tok_rows = queries.shape[0]
    row_width = queries.shape[1]
    head_dim = key_rows.shape[1]
    head_count = row_width // head_dim
    chip_count = lax.axis_size("chip")
    chip = lax.axis_index("chip")
    core = lax.axis_index("core")
    lead = core == 0
    score_scale = 1.0 / math.sqrt(head_dim)
    pass_rates = pass_rate(correct, group_size)
    traces = jnp.arange(pass_rates.shape[0], dtype=jnp.int32)
    weights = jnp.sum(
        jnp.where(trace_ids[:, None] == traces[None, :], pass_rates[None, :], 0.0), axis=1
    )
    out_grads = (weights[:, None] * cotangent.astype(jnp.float32)).astype(jnp.bfloat16)

    joined = jnp.concatenate([key_rows, value_rows], 1)
    spread = jnp.broadcast_to(joined[None], (chip_count,) + joined.shape)
    mine = lax.all_to_all(spread, "chip", 0, 0, tiled=True).reshape(chip_count * tok_rows, 2 * head_dim)
    own = jnp.concatenate([queries, out_grads], 1)
    partner = lax.ppermute(own, "core", [(0, 1), (1, 0)])

    rows = 2 * head_count * tok_rows
    vmem = pl.BlockSpec(memory_space=pltpu.MemorySpace.VMEM)
    smem = pl.BlockSpec(memory_space=pltpu.MemorySpace.SMEM)
    settings = dict(
        heads=head_count, head_dim=head_dim, tok_rows=tok_rows, score_scale=score_scale,
        tile_chips=math.gcd(chip_count, 4),
    )
    index = jnp.stack([chip, core]).astype(jnp.int32)
    stats = pl.pallas_call(
        functools.partial(forward_kernel, **settings),
        out_shape=jax.ShapeDtypeStruct((8, rows), jnp.float32),
        in_specs=[smem, vmem, vmem, vmem],
        out_specs=vmem,
    )(index, own, partner, mine)
    partner_stats = lax.ppermute(stats, "core", [(0, 1), (1, 0)])
    log_totals, query_grads, own_part = pl.pallas_call(
        functools.partial(backward_kernel, **settings),
        out_shape=(
            jax.ShapeDtypeStruct((1, rows), jnp.float32),
            jax.ShapeDtypeStruct((2 * tok_rows, row_width), jnp.float32),
            jax.ShapeDtypeStruct((chip_count * tok_rows, 2 * head_dim), jnp.float32),
        ),
        in_specs=[smem, vmem, vmem, vmem, vmem, vmem],
        out_specs=(vmem, vmem, vmem),
    )(index, own, partner, mine, stats, partner_stats)

    reduced = jnp.sum(
        lax.all_to_all(own_part.reshape(chip_count, tok_rows, 2 * head_dim), "chip", 0, 0, tiled=True),
        axis=0,
    )
    grad_keys = reduced[:, :head_dim].astype(jnp.bfloat16)
    grad_values = reduced[:, head_dim:].astype(jnp.bfloat16)
    mine_dq = jnp.where(lead, query_grads[:tok_rows], query_grads[tok_rows:])
    other_dq = jnp.where(lead, query_grads[tok_rows:], query_grads[:tok_rows])
    query_grads = mine_dq + lax.ppermute(other_dq, "core", [(0, 1), (1, 0)])
    half = head_count * tok_rows
    own_totals = jnp.where(lead, log_totals[:, :half], log_totals[:, half:]) * LN_2
    log_totals = own_totals.reshape(head_count, tok_rows).T
    return (log_totals, query_grads, grad_keys, grad_values)


def solution(mesh):
    order = [mesh.axis_names.index("ctx"), mesh.axis_names.index("head")]
    devices = mesh.devices.transpose(order)
    ctx_size, head_size = devices.shape
    chip_mesh = Mesh(devices.reshape(ctx_size // 2, 2, head_size), ("chip", "core", "head"))
    rows = P(("chip", "core"), "head")
    return jax.shard_map(
        body,
        mesh=chip_mesh,
        in_specs=(rows, rows, rows, rows, P(("chip", "core")), P(), P()),
        out_specs=(rows, rows, rows, rows),
        check_vma=False,
    )
```
